256 devices in a mesh: pipe: 2 (over x_hi), ctx: 16 (over y, x_lo, core), dp: 8 (over z).
Axes of the slice: x: 4 (x_hi: 2, x_lo: 2; x = x_hi * 2 + x_lo), y: 4, z: 8, core: 2. Of those that a mesh axis runs over, the one named last changes fastest.
Arguments:
- patches: bfloat16 [1, 8, 2048, 1024], P(None, 'dp', 'ctx'), may hold values from -6 to 6
- lengths: int32 [1, 8], P(None, 'dp'), may hold values from 512 to 2048, as said below
- norm_gain: float32 [2, 1024], P('pipe'), may hold values from 0.1 to 1.9
- norm_bias: float32 [2, 1024], P('pipe'), may hold values from -3 to 3
- w_qkv: bfloat16 [2, 1024, 3072], P('pipe', None, 'dp')
- w_out: bfloat16 [2, 1024, 1024], P('pipe'), may hold values from -0.1875 to 0.1875
- out_bias: float32 [2, 1024], P('pipe'), may hold values from -3 to 3
- scale_gain: float32 [2, 1024], P('pipe'), may hold values from 0.3 to 1.5
Outputs:
- section_outputs: bfloat16 [2, 1, 8, 2048, 1024], P('pipe', None, 'dp', 'ctx')
The draws below stay inside these ranges and needn't reach their ends.
Inputs may be any that keep to these rules, and one draw needn't show every extreme that they name: `lengths`: every volume has at least 512 real tokens, and in every draw some volume fills all 2048 slots.
All inputs are finite; a program needn't handle non-finite values.
Results may differ from the reference program's by a relative error of at most 0.017.
The reference program's roundings to bfloat16 on the way count: a program that leaves them out, or rounds other values in their place, can miss the bound.
Values may be sent and summed in bfloat16 or wider, within the bound.
No kernel may reach another device: no remote copies, remote signals or barrier semaphores. Data moves between devices by JAX's collectives and lax.ppermute only.
A program may use at most 128 MiB of HBM per device.

```python
import math
import jax
import jax.numpy as jnp
from jax import lax

D = 1024
HEADS = 16
HEAD_DIM = 64
MICRO = 1
SEQ = 2048
VOLUMES = 8
N_PIPE = 2


def draw_lengths(key, part):
    total_count = MICRO * VOLUMES
    drawn = jax.random.randint(key, (total_count,), SEQ // 4, SEQ + 1)
    chosen = jax.random.randint(jax.random.fold_in(key, 7), (), 0, total_count)
    drawn = jnp.where(jnp.arange(total_count) == chosen, SEQ, drawn)
    return drawn.reshape(MICRO, VOLUMES).astype(jnp.int32)


def draw_w_qkv(key, part):
    base_scale = math.sqrt(2.0 / D)
    first_key = jax.random.fold_in(key, 0)
    third_key = jax.random.fold_in(key, 2)
    fourth_key = jax.random.fold_in(key, 3)
    query_part = jax.random.normal(first_key, (N_PIPE, D, D), jnp.float32) * base_scale
    key_part = jax.random.normal(fourth_key, (N_PIPE, D, D), jnp.float32) * base_scale
    value_part = jax.random.normal(third_key, (N_PIPE, D, D), jnp.float32) * base_scale
    return jnp.concatenate([query_part, key_part, value_part], axis=-1).astype(jnp.bfloat16)


def block_levels(stream_key, dims, cuts, smallest, largest):
    level, own = 1.0, jax.random.fold_in(stream_key, 6)
    for axis_at, shards_of in cuts:
        steps = jnp.exp(jax.random.uniform(jax.random.fold_in(own, axis_at), (shards_of,), jnp.float32, smallest / len(cuts), largest / len(cuts)))
        level = level * jnp.repeat(steps, dims[axis_at] // shards_of).reshape([-1 if axis == axis_at else 1 for axis in range(len(dims))])
    return level


def normal_values(own_key, dims, deviation, reach, cuts=(), held_as=jnp.bfloat16):
    array = jax.random.normal(own_key, dims, jnp.float32) * deviation
    if len(cuts) > 0:
        array = block_levels(own_key, dims, cuts, -0.22, 0.18) * array
    return jnp.clip(array, min=-reach, max=reach).astype(held_as)


def setup_inputs(seed: int = 0) -> dict:
    streams_of = jax.random.split(jax.random.key(seed), 9)
    return {
        "patches": normal_values(streams_of[0], (MICRO, VOLUMES, SEQ, D), 1.0, 6.0, ((1, 8), (2, 16))),
        "lengths": draw_lengths(jax.random.fold_in(streams_of[8], 71), 0),
        "norm_gain": jnp.clip(1.0 + 0.18 * jax.random.normal(streams_of[2], (N_PIPE, D), jnp.float32), 0.1, 1.9),
        "norm_bias": normal_values(streams_of[3], (N_PIPE, D), 0.5, 3.0, ((0, 2),), jnp.float32),
        "w_qkv": draw_w_qkv(jax.random.fold_in(streams_of[8], 71), 0),
        "w_out": normal_values(streams_of[5], (N_PIPE, D, D), D ** -0.5, 0.1875, ((0, 2),)),
        "out_bias": normal_values(streams_of[6], (N_PIPE, D), 0.5, 3.0, ((0, 2),), jnp.float32),
        "scale_gain": jnp.clip(jnp.exp(math.log(1.5) - 1.60943787 * jax.random.uniform(streams_of[7], (N_PIPE, D), jnp.float32) ** block_levels(streams_of[7], (N_PIPE, D), ((0, 2),), -0.2, 0.2)), 0.3, 1.5),
    }


epsilon = 1e-06
masked_score = -1e+30

def normalize(hidden, gain, shift):
    values = hidden.astype(jnp.float32)
    row_mean = lax.optimization_barrier(jnp.mean(values, axis=-1, keepdims=True))
    centered = values - row_mean
    variance = lax.optimization_barrier(jnp.mean(centered * centered, axis=-1, keepdims=True))
    return (centered * lax.rsqrt(variance + epsilon) * gain + shift).astype(jnp.bfloat16)

def sublayer(hidden, length, gain, shift, qkv_weight, out_weight, out_shift, layer_scale):
    normed = normalize(hidden, gain, shift)
    projected = jnp.dot(normed, qkv_weight, preferred_element_type=jnp.float32).astype(jnp.bfloat16)
    projected = projected.reshape(SEQ, 3, HEADS, HEAD_DIM)
    queries = projected[:, 0].astype(jnp.float32)
    key_rows = projected[:, 1].astype(jnp.float32)
    value_rows = projected[:, 2].astype(jnp.float32)
    scores = jnp.einsum('qhd,khd->hqk', queries, key_rows) * HEAD_DIM ** (-0.5)
    valid = jnp.arange(SEQ, dtype=jnp.int32) < length
    scores = jnp.where(valid[None, None, :], scores, masked_score)
    top_score = lax.optimization_barrier(jnp.max(scores, axis=-1, keepdims=True))
    weights = jnp.where(valid[None, None, :], jnp.exp(scores - top_score), 0.0)
    totals = lax.optimization_barrier(jnp.sum(weights, axis=-1))
    rounded = lax.optimization_barrier(weights.astype(jnp.bfloat16)).astype(jnp.float32)
    context = jnp.einsum('hqk,khd->qhd', rounded, value_rows) / totals.T[:, :, None]
    context = context.astype(jnp.bfloat16).reshape(SEQ, D)
    mixed = jnp.dot(context, out_weight, preferred_element_type=jnp.float32) + out_shift
    return (hidden.astype(jnp.float32) + layer_scale * mixed).astype(jnp.bfloat16)

def reference(patches, lengths, norm_gain, norm_bias, w_qkv, w_out, out_bias, scale_gain):
    current = patches.reshape(MICRO * VOLUMES, SEQ, D)
    flat_lengths = lengths.reshape(MICRO * VOLUMES)
    collected = []
    for layer_index in range(N_PIPE):

        def run_volume(item, layer_index=layer_index):
            return sublayer(item[0], item[1], norm_gain[layer_index], norm_bias[layer_index], w_qkv[layer_index], w_out[layer_index], out_bias[layer_index], scale_gain[layer_index])
        current = lax.map(run_volume, (current, flat_lengths))
        collected.append(current.reshape(MICRO, VOLUMES, SEQ, D))
    return jnp.stack(collected)
```

```python
import jax
import jax.numpy as jnp
from jax import lax
from jax.sharding import PartitionSpec as P

HEADS = 16


epsilon = 1e-06
masked_score = -1e30


def normalize(hidden, gain, shift):
    values = hidden.astype(jnp.float32)
    row_mean = jnp.mean(values, axis=-1, keepdims=True)
    centered = values - row_mean
    variance = jnp.mean(centered * centered, axis=-1, keepdims=True)
    return (centered * lax.rsqrt(variance + epsilon) * gain + shift).astype(jnp.bfloat16)


def head_attention(qkv, length, score_scale):
    queries = qkv[:, :, 0]
    key_rows = qkv[:, :, 1]
    value_rows = qkv[:, :, 2]
    count = qkv.shape[1]
    scores = (
        jnp.einsum("hqd,hkd->hqk", queries, key_rows, preferred_element_type=jnp.float32)
        * score_scale
    )
    valid = jnp.arange(count, dtype=jnp.int32) < length
    top = jnp.max(jnp.where(valid[None, None, :], scores, masked_score), axis=-1)
    weights = jnp.where(valid[None, None, :], jnp.exp(scores - top[:, :, None]), 0.0)
    totals = jnp.sum(weights, axis=-1)
    context = jnp.einsum(
        "hqk,hkd->hqd",
        weights.astype(jnp.bfloat16),
        value_rows,
        preferred_element_type=jnp.float32,
    )
    return (context / totals[:, :, None]).astype(jnp.bfloat16)


def sublayer(current, length, qkv_full, out_full, gain, shift, out_shift, layer_scale):
    tok_rows, width = current.shape
    head_width = width // HEADS
    ctx_count = lax.axis_size("ctx")
    heads_here = HEADS // ctx_count
    normed = normalize(current, gain, shift)
    weight = qkv_full.reshape(width, 3, HEADS, head_width)
    projected = jnp.einsum(
        "tk,kphf->htpf", normed, weight, preferred_element_type=jnp.float32
    ).astype(jnp.bfloat16)
    gathered = lax.all_to_all(projected, "ctx", 0, 1, tiled=True)
    context = head_attention(gathered, length, head_width ** (-0.5))
    spread = lax.all_to_all(context, "ctx", 1, 0, tiled=True)
    spread = jnp.transpose(spread, (1, 0, 2)).reshape(tok_rows, width)
    mixed = jnp.dot(spread, out_full, preferred_element_type=jnp.float32) + out_shift
    return (current.astype(jnp.float32) + layer_scale * mixed).astype(jnp.bfloat16)


def per_device(patches, lengths, norm_gain, norm_bias, w_qkv, w_out, out_bias, scale_gain):
    section_index = lax.axis_index("pipe")
    section_count = lax.axis_size("pipe")
    qkv_full = lax.all_gather(w_qkv[0], "dp", axis=1, tiled=True)
    args = (qkv_full, w_out[0], norm_gain[0], norm_bias[0], out_bias[0], scale_gain[0])
    length = lengths[0, 0]
    current = patches[0, 0]
    outputs = []
    for turn_index in range(section_count):
        produced = sublayer(current, length, *args)
        outputs.append(produced)
        if turn_index + 1 < section_count:
            pairs = [(i, i + 1) for i in range(section_count - 1)]
            current = lax.ppermute(produced, "pipe", pairs)
    result = outputs[0]
    for turn_index in range(1, section_count):
        result = jnp.where(section_index == turn_index, outputs[turn_index], result)
    return result[None, None, None]


def solution(mesh):
    in_specs = (
        P(None, "dp", "ctx", None),
        P(None, "dp"),
        P("pipe", None),
        P("pipe", None),
        P("pipe", None, "dp"),
        P("pipe", None, None),
        P("pipe", None),
        P("pipe", None),
    )
    out_specs = P("pipe", None, "dp", "ctx", None)
    return jax.shard_map(
        per_device, mesh=mesh, in_specs=in_specs, out_specs=out_specs, check_vma=False
    )
```

```python
import jax
import jax.numpy as jnp
from jax import lax
from jax.sharding import PartitionSpec as P

HEADS = 16


epsilon = 1e-06
masked_score = -1e30


def normalize(hidden, gain, shift):
    values = hidden.astype(jnp.float32)
    row_mean = jnp.mean(values, axis=-1, keepdims=True)
    centered = values - row_mean
    variance = jnp.mean(centered * centered, axis=-1, keepdims=True)
    return (centered * lax.rsqrt(variance + epsilon) * gain + shift).astype(jnp.bfloat16)


def head_attention(qkv, length, score_scale):
    queries, key_rows, value_rows = qkv[0], qkv[1], qkv[2]
    count = qkv.shape[-1]
    scores = (
        jnp.einsum("dq,dk->qk", queries, key_rows, preferred_element_type=jnp.float32)
        * score_scale
    )
    valid = jnp.arange(count, dtype=jnp.int32) < length
    top = jnp.max(jnp.where(valid[None, :], scores, masked_score), axis=-1)
    weights = jnp.where(valid[None, :], jnp.exp(scores - top[:, None]), 0.0)
    totals = jnp.sum(weights, axis=-1)
    context = jnp.einsum(
        "qk,dk->dq", weights.astype(jnp.bfloat16), value_rows, preferred_element_type=jnp.float32
    )
    return (context / totals[None, :]).astype(jnp.bfloat16)


def sublayer(current, length, qkv_mine, qkv_other, out_full, gain, shift, out_shift, layer_scale):
    tok_rows, width = current.shape
    head_width = width // HEADS
    ctx_count = lax.axis_size("ctx")
    core = lax.axis_index("ctx") % 2
    half = width // 2
    normed = normalize(current, gain, shift)
    normed_mine = lax.dynamic_slice_in_dim(normed, core * half, half, axis=1)
    normed_other = lax.dynamic_slice_in_dim(normed, (1 - core) * half, half, axis=1)
    projected = jnp.einsum(
        "tk,kphf->hpft", normed_mine, qkv_mine.reshape(half, 3, HEADS, head_width),
        preferred_element_type=jnp.float32,
    ) + jnp.einsum(
        "tk,kphf->hpft", normed_other, qkv_other.reshape(half, 3, HEADS, head_width),
        preferred_element_type=jnp.float32,
    )
    projected = projected.astype(jnp.bfloat16)
    gathered = lax.all_to_all(projected, "ctx", 0, 3, tiled=True)
    context = head_attention(gathered[0], length, head_width ** (-0.5))
    context = jnp.transpose(context.reshape(head_width, ctx_count, tok_rows), (1, 0, 2))
    spread = lax.all_to_all(context, "ctx", 0, 0, tiled=True).reshape(width, tok_rows)
    mixed = jnp.einsum("ft,fo->to", spread, out_full, preferred_element_type=jnp.float32)
    mixed = mixed + out_shift
    return (current.astype(jnp.float32) + layer_scale * mixed).astype(jnp.bfloat16)


def per_device(patches, lengths, norm_gain, norm_bias, w_qkv, w_out, out_bias, scale_gain):
    section_index = lax.axis_index("pipe")
    section_count = lax.axis_size("pipe")
    core = lax.axis_index("ctx") % 2
    width = w_qkv.shape[1]
    half = width // 2
    rows_mine = lax.dynamic_slice_in_dim(w_qkv[0], core * half, half, axis=0)
    qkv_mine = lax.all_gather(rows_mine, "dp", axis=1, tiled=True)
    sibling = [(i, i ^ 1) for i in range(lax.axis_size("ctx"))]
    qkv_other = lax.ppermute(qkv_mine, "ctx", sibling)
    args = (qkv_mine, qkv_other, w_out[0], norm_gain[0], norm_bias[0], out_bias[0], scale_gain[0])
    length = lengths[0, 0]
    current = patches[0, 0]
    outputs = []
    for turn_index in range(section_count):
        produced = sublayer(current, length, *args)
        outputs.append(produced)
        if turn_index + 1 < section_count:
            pairs = [(i, i + 1) for i in range(section_count - 1)]
            current = lax.ppermute(produced, "pipe", pairs)
    result = outputs[0]
    for turn_index in range(1, section_count):
        result = jnp.where(section_index == turn_index, outputs[turn_index], result)
    return result[None, None, None]


def solution(mesh):
    in_specs = (
        P(None, "dp", "ctx", None),
        P(None, "dp"),
        P("pipe", None),
        P("pipe", None),
        P("pipe", None, "dp"),
        P("pipe", None, None),
        P("pipe", None),
        P("pipe", None),
    )
    out_specs = P("pipe", None, "dp", "ctx", None)
    return jax.shard_map(
        per_device, mesh=mesh, in_specs=in_specs, out_specs=out_specs, check_vma=False
    )
```

```python
import jax
import jax.numpy as jnp
from jax import lax
from jax.sharding import PartitionSpec as P

HEADS = 16


epsilon = 1e-06
masked_score = -1e30


def normalize(hidden, gain, shift):
    values = hidden.astype(jnp.float32)
    row_mean = jnp.mean(values, axis=-1, keepdims=True)
    centered = values - row_mean
    variance = jnp.mean(centered * centered, axis=-1, keepdims=True)
    return (centered * lax.rsqrt(variance + epsilon) * gain + shift).astype(jnp.bfloat16)


def head_attention(qkv, length, score_scale):
    queries, key_rows, value_rows = qkv[0], qkv[1], qkv[2]
    count = qkv.shape[-1]
    scores = (
        jnp.einsum("dq,dk->qk", queries, key_rows, preferred_element_type=jnp.float32)
        * score_scale
    )
    valid = jnp.arange(count, dtype=jnp.int32) < length
    top = jnp.max(jnp.where(valid[None, :], scores, masked_score), axis=-1)
    weights = jnp.where(valid[None, :], jnp.exp(scores - top[:, None]), 0.0)
    totals = jnp.sum(weights, axis=-1)
    context = jnp.einsum(
        "qk,dk->dq", weights.astype(jnp.bfloat16), value_rows, preferred_element_type=jnp.float32
    )
    return (context / totals[None, :]).astype(jnp.bfloat16)


def chunk_tables(width, dp_count, chunks, head_width):
    shard_width = 3 * width // dp_count
    chunk_width = shard_width // chunks
    per_segment = chunk_width // head_width
    orders, parts = [], []
    for j in range(chunks):
        by_head = {}
        for d in range(dp_count):
            for i in range(per_segment):
                column = d * shard_width + j * chunk_width + i * head_width
                part, head = column // width, (column % width) // head_width
                assert head not in by_head
                by_head[head] = (d * per_segment + i, part)
        assert sorted(by_head) == list(range(HEADS))
        orders.append([by_head[h][0] for h in range(HEADS)])
        parts.append([by_head[h][1] for h in range(HEADS)])
    chunk_of_part = [[parts_h.index(p) for p in range(3)] for parts_h in zip(*parts)]
    return orders, chunk_of_part


def sublayer(current, length, weights_mine, weights_other, orders, chunk_of_part, out_full,
             gain, shift, out_shift, layer_scale):
    tok_rows, width = current.shape
    head_width = width // HEADS
    ctx_count = lax.axis_size("ctx")
    assert ctx_count == HEADS
    head = lax.axis_index("ctx")
    core = head % 2
    half = width // 2
    normed = normalize(current, gain, shift)
    normed_mine = lax.dynamic_slice_in_dim(normed, core * half, half, axis=1)
    normed_other = lax.dynamic_slice_in_dim(normed, (1 - core) * half, half, axis=1)
    received = []
    for mine, other, order in zip(weights_mine, weights_other, orders):
        projected = jnp.dot(normed_mine, mine, preferred_element_type=jnp.float32) + jnp.dot(
            normed_other, other, preferred_element_type=jnp.float32
        )
        projected = projected.astype(jnp.bfloat16).reshape(tok_rows, -1, head_width)
        projected = jnp.transpose(projected, (1, 2, 0))
        by_head = jnp.concatenate([projected[k : k + 1] for k in order], axis=0)
        received.append(lax.all_to_all(by_head, "ctx", 0, 2, tiled=True)[0])
    received = jnp.stack(received)
    pick = jnp.asarray(chunk_of_part, jnp.int32)[head]
    qkv = jnp.take(received, pick, axis=0)
    context = head_attention(qkv, length, head_width ** (-0.5))
    context = jnp.transpose(context.reshape(head_width, ctx_count, tok_rows), (1, 0, 2))
    spread = lax.all_to_all(context, "ctx", 0, 0, tiled=True).reshape(width, tok_rows)
    mixed = jnp.einsum("ft,fo->to", spread, out_full, preferred_element_type=jnp.float32)
    mixed = mixed + out_shift
    return (current.astype(jnp.float32) + layer_scale * mixed).astype(jnp.bfloat16)


def per_device(patches, lengths, norm_gain, norm_bias, w_qkv, w_out, out_bias, scale_gain):
    section_index = lax.axis_index("pipe")
    section_count = lax.axis_size("pipe")
    dp_count = lax.axis_size("dp")
    core = lax.axis_index("ctx") % 2
    width = w_qkv.shape[1]
    half = width // 2
    head_width = width // HEADS
    chunks = 3
    orders, chunk_of_part = chunk_tables(width, dp_count, chunks, head_width)
    rows_mine = lax.dynamic_slice_in_dim(w_qkv[0], core * half, half, axis=0)
    chunk_width = rows_mine.shape[1] // chunks
    sibling = [(i, i ^ 1) for i in range(lax.axis_size("ctx"))]
    weights_mine, weights_other = [], []
    for j in range(chunks):
        piece = rows_mine[:, j * chunk_width : (j + 1) * chunk_width]
        gathered = lax.all_gather(piece, "dp", axis=1, tiled=True)
        weights_mine.append(gathered)
        weights_other.append(lax.ppermute(gathered, "ctx", sibling))
    args = (weights_mine, weights_other, orders, chunk_of_part, w_out[0], norm_gain[0],
            norm_bias[0], out_bias[0], scale_gain[0])
    length = lengths[0, 0]
    current = patches[0, 0]
    outputs = []
    for turn_index in range(section_count):
        produced = sublayer(current, length, *args)
        outputs.append(produced)
        if turn_index + 1 < section_count:
            pairs = [(i, i + 1) for i in range(section_count - 1)]
            current = lax.ppermute(produced, "pipe", pairs)
    result = outputs[0]
    for turn_index in range(1, section_count):
        result = jnp.where(section_index == turn_index, outputs[turn_index], result)
    return result[None, None, None]


def solution(mesh):
    in_specs = (
        P(None, "dp", "ctx", None),
        P(None, "dp"),
        P("pipe", None),
        P("pipe", None),
        P("pipe", None, "dp"),
        P("pipe", None, None),
        P("pipe", None),
        P("pipe", None),
    )
    out_specs = P("pipe", None, "dp", "ctx", None)
    return jax.shard_map(
        per_device, mesh=mesh, in_specs=in_specs, out_specs=out_specs, check_vma=False
    )
```

```python
import jax
import jax.numpy as jnp
from jax import lax
from jax.sharding import PartitionSpec as P

HEADS = 16


epsilon = 1e-06
masked_score = -1e30


def normalize(hidden, gain, shift):
    values = hidden.astype(jnp.float32)
    row_mean = jnp.mean(values, axis=-1, keepdims=True)
    centered = values - row_mean
    variance = jnp.mean(centered * centered, axis=-1, keepdims=True)
    return (centered * lax.rsqrt(variance + epsilon) * gain + shift).astype(jnp.bfloat16)


def head_attention(qkv, length, score_scale):
    queries, key_rows, value_rows = qkv[0], qkv[1], qkv[2]
    count = qkv.shape[-1]
    scores = (
        jnp.einsum("dq,dk->qk", queries, key_rows, preferred_element_type=jnp.float32)
        * score_scale
    )
    valid = jnp.arange(count, dtype=jnp.int32) < length
    top = jnp.max(jnp.where(valid[None, :], scores, masked_score), axis=-1)
    weights = jnp.where(valid[None, :], jnp.exp(scores - top[:, None]), 0.0)
    totals = jnp.sum(weights, axis=-1)
    context = jnp.einsum(
        "qk,dk->dq", weights.astype(jnp.bfloat16), value_rows, preferred_element_type=jnp.float32
    )
    return (context / totals[None, :]).astype(jnp.bfloat16)


def sublayer(current, length, qkv_mine, qkv_other, out_full, gain, shift, out_shift, layer_scale):
    tok_rows, width = current.shape
    head_width = width // HEADS
    ctx_count = lax.axis_size("ctx")
    core = lax.axis_index("ctx") % 2
    half = width // 2
    normed = normalize(current, gain, shift)
    normed_mine = lax.dynamic_slice_in_dim(normed, core * half, half, axis=1)
    normed_other = lax.dynamic_slice_in_dim(normed, (1 - core) * half, half, axis=1)
    projected = jnp.dot(normed_mine, qkv_mine, preferred_element_type=jnp.float32) + jnp.dot(
        normed_other, qkv_other, preferred_element_type=jnp.float32
    )
    projected = jnp.transpose(projected.reshape(tok_rows, 3, HEADS, head_width), (2, 1, 3, 0))
    projected = projected.astype(jnp.bfloat16)
    gathered = lax.all_to_all(projected, "ctx", 0, 3, tiled=True)
    context = head_attention(gathered[0], length, head_width ** (-0.5))
    context = jnp.transpose(context.reshape(head_width, ctx_count, tok_rows), (1, 0, 2))
    spread = lax.all_to_all(context, "ctx", 0, 0, tiled=True).reshape(width, tok_rows)
    mixed = jnp.einsum("ft,fo->to", spread, out_full, preferred_element_type=jnp.float32)
    mixed = mixed + out_shift
    return (current.astype(jnp.float32) + layer_scale * mixed).astype(jnp.bfloat16)


def per_device(patches, lengths, norm_gain, norm_bias, w_qkv, w_out, out_bias, scale_gain):
    section_index = lax.axis_index("pipe")
    section_count = lax.axis_size("pipe")
    core = lax.axis_index("ctx") % 2
    width = w_qkv.shape[1]
    half = width // 2
    rows_mine = lax.dynamic_slice_in_dim(w_qkv[0], core * half, half, axis=0)
    qkv_mine = lax.all_gather(rows_mine, "dp", axis=1, tiled=True)
    sibling = [(i, i ^ 1) for i in range(lax.axis_size("ctx"))]
    qkv_other = lax.ppermute(qkv_mine, "ctx", sibling)
    args = (qkv_mine, qkv_other, w_out[0], norm_gain[0], norm_bias[0], out_bias[0], scale_gain[0])
    length = lengths[0, 0]
    current = patches[0, 0]
    outputs = []
    for turn_index in range(section_count):
        produced = sublayer(current, length, *args)
        outputs.append(produced)
        if turn_index + 1 < section_count:
            pairs = [(i, i + 1) for i in range(section_count - 1)]
            current = lax.ppermute(produced, "pipe", pairs)
    result = outputs[0]
    for turn_index in range(1, section_count):
        result = jnp.where(section_index == turn_index, outputs[turn_index], result)
    return result[None, None, None]


def solution(mesh):
    in_specs = (
        P(None, "dp", "ctx", None),
        P(None, "dp"),
        P("pipe", None),
        P("pipe", None),
        P("pipe", None, "dp"),
        P("pipe", None, None),
        P("pipe", None),
        P("pipe", None),
    )
    out_specs = P("pipe", None, "dp", "ctx", None)
    return jax.shard_map(
        per_device, mesh=mesh, in_specs=in_specs, out_specs=out_specs, check_vma=False
    )
```

```python
import jax
import jax.numpy as jnp
from jax import lax
from jax.sharding import PartitionSpec as P

HEADS = 16


epsilon = 1e-06
masked_score = -1e30


def normalize(hidden, gain, shift):
    values = hidden.astype(jnp.float32)
    row_mean = jnp.mean(values, axis=-1, keepdims=True)
    centered = values - row_mean
    variance = jnp.mean(centered * centered, axis=-1, keepdims=True)
    return (centered * lax.rsqrt(variance + epsilon) * gain + shift).astype(jnp.bfloat16)


def head_attention(qkv, length, score_scale):
    queries, key_rows, value_rows = qkv[0], qkv[1], qkv[2]
    count = qkv.shape[-1]
    scores = (
        jnp.einsum("dq,dk->qk", queries, key_rows, preferred_element_type=jnp.float32)
        * score_scale
    )
    valid = jnp.arange(count, dtype=jnp.int32) < length
    top = jnp.max(jnp.where(valid[None, :], scores, masked_score), axis=-1)
    weights = jnp.where(valid[None, :], jnp.exp(scores - top[:, None]), 0.0)
    totals = jnp.sum(weights, axis=-1)
    context = jnp.einsum(
        "qk,dk->dq", weights.astype(jnp.bfloat16), value_rows, preferred_element_type=jnp.float32
    )
    return (context / totals[None, :]).astype(jnp.bfloat16)


def sublayer(current, length, qkv_mine, qkv_other, out_full, gain, shift, out_shift, layer_scale):
    tok_rows, width = current.shape
    head_width = width // HEADS
    ctx_count = lax.axis_size("ctx")
    core = lax.axis_index("ctx") % 2
    half = width // 2
    normed = normalize(current, gain, shift)
    normed_mine = lax.dynamic_slice_in_dim(normed, core * half, half, axis=1)
    normed_other = lax.dynamic_slice_in_dim(normed, (1 - core) * half, half, axis=1)
    projected = jnp.dot(normed_mine, qkv_mine, preferred_element_type=jnp.float32) + jnp.dot(
        normed_other, qkv_other, preferred_element_type=jnp.float32
    )
    projected = jnp.transpose(projected.reshape(tok_rows, 3, HEADS, head_width), (2, 1, 3, 0))
    projected = projected.astype(jnp.bfloat16)
    gathered = lax.all_to_all(projected, "ctx", 0, 3, tiled=True)
    context = head_attention(gathered[0], length, head_width ** (-0.5))
    context = jnp.transpose(context.reshape(head_width, ctx_count, tok_rows), (1, 0, 2))
    spread = lax.all_to_all(context, "ctx", 0, 0, tiled=True).reshape(width, tok_rows)
    mixed = jnp.einsum("ft,fo->to", spread, out_full, preferred_element_type=jnp.float32)
    mixed = mixed + out_shift
    return (current.astype(jnp.float32) + layer_scale * mixed).astype(jnp.bfloat16)


def ring_gather(piece, axis):
    count = lax.axis_size(axis)
    index = lax.axis_index(axis)
    rows, cols = piece.shape
    whole = jnp.zeros((rows, cols * count), piece.dtype)
    whole = lax.dynamic_update_slice_in_dim(whole, piece, index * cols, axis=1)
    right = [(i, (i + 1) % count) for i in range(count)]
    left = [(i, (i - 1) % count) for i in range(count)]
    forward, backward = piece, piece
    for step in range(count // 2):
        forward = lax.ppermute(forward, axis, right)
        owner = (index - 1 - step) % count
        whole = lax.dynamic_update_slice_in_dim(whole, forward, owner * cols, axis=1)
        if step < (count - 1) // 2:
            backward = lax.ppermute(backward, axis, left)
            owner = (index + 1 + step) % count
            whole = lax.dynamic_update_slice_in_dim(whole, backward, owner * cols, axis=1)
    return whole


def per_device(patches, lengths, norm_gain, norm_bias, w_qkv, w_out, out_bias, scale_gain):
    section_index = lax.axis_index("pipe")
    section_count = lax.axis_size("pipe")
    core = lax.axis_index("ctx") % 2
    width = w_qkv.shape[1]
    half = width // 2
    rows_mine = lax.dynamic_slice_in_dim(w_qkv[0], core * half, half, axis=0)
    qkv_mine = ring_gather(rows_mine, "dp")
    sibling = [(i, i ^ 1) for i in range(lax.axis_size("ctx"))]
    qkv_other = lax.ppermute(qkv_mine, "ctx", sibling)
    args = (qkv_mine, qkv_other, w_out[0], norm_gain[0], norm_bias[0], out_bias[0], scale_gain[0])
    length = lengths[0, 0]
    current = patches[0, 0]
    outputs = []
    for turn_index in range(section_count):
        produced = sublayer(current, length, *args)
        outputs.append(produced)
        if turn_index + 1 < section_count:
            pairs = [(i, i + 1) for i in range(section_count - 1)]
            current = lax.ppermute(produced, "pipe", pairs)
    result = outputs[0]
    for turn_index in range(1, section_count):
        result = jnp.where(section_index == turn_index, outputs[turn_index], result)
    return result[None, None, None]


def solution(mesh):
    in_specs = (
        P(None, "dp", "ctx", None),
        P(None, "dp"),
        P("pipe", None),
        P("pipe", None),
        P("pipe", None, "dp"),
        P("pipe", None, None),
        P("pipe", None),
        P("pipe", None),
    )
    out_specs = P("pipe", None, "dp", "ctx", None)
    return jax.shard_map(
        per_device, mesh=mesh, in_specs=in_specs, out_specs=out_specs, check_vma=False
    )
```

```python
import jax
import jax.numpy as jnp
from jax import lax
from jax.sharding import PartitionSpec as P

HEADS = 16


epsilon = 1e-06
masked_score = -1e30


def normalize(hidden, gain, shift):
    values = hidden.astype(jnp.float32)
    row_mean = jnp.mean(values, axis=-1, keepdims=True)
    centered = values - row_mean
    variance = jnp.mean(centered * centered, axis=-1, keepdims=True)
    return (centered * lax.rsqrt(variance + epsilon) * gain + shift).astype(jnp.bfloat16)


def head_attention(qkv, length, score_scale):
    queries, key_rows, value_rows = qkv[0], qkv[1], qkv[2]
    count = qkv.shape[-1]
    scores = (
        jnp.einsum("dq,dk->qk", queries, key_rows, preferred_element_type=jnp.float32)
        * score_scale
    )
    valid = jnp.arange(count, dtype=jnp.int32) < length
    top = jnp.max(jnp.where(valid[None, :], scores, masked_score), axis=-1)
    weights = jnp.where(valid[None, :], jnp.exp(scores - top[:, None]), 0.0)
    totals = jnp.sum(weights, axis=-1)
    context = jnp.einsum(
        "qk,dk->dq", weights.astype(jnp.bfloat16), value_rows, preferred_element_type=jnp.float32
    )
    return (context / totals[None, :]).astype(jnp.bfloat16)


def sublayer(current, length, qkv_mine, qkv_other, out_full, gain, shift, out_shift, layer_scale,
             projected=None):
    tok_rows, width = current.shape
    head_width = width // HEADS
    ctx_count = lax.axis_size("ctx")
    core = lax.axis_index("ctx") % 2
    half = width // 2
    if projected is None:
        normed = normalize(current, gain, shift)
        normed_mine = lax.dynamic_slice_in_dim(normed, core * half, half, axis=1)
        normed_other = lax.dynamic_slice_in_dim(normed, (1 - core) * half, half, axis=1)
        projected = jnp.dot(normed_mine, qkv_mine, preferred_element_type=jnp.float32) + jnp.dot(
            normed_other, qkv_other, preferred_element_type=jnp.float32
        )
        projected = unrotate(projected.astype(jnp.bfloat16), "dp")
    projected = jnp.transpose(projected.reshape(tok_rows, 3, HEADS, head_width), (2, 1, 3, 0))
    gathered = lax.all_to_all(projected, "ctx", 0, 3, tiled=True)
    context = head_attention(gathered[0], length, head_width ** (-0.5))
    context = jnp.transpose(context.reshape(head_width, ctx_count, tok_rows), (1, 0, 2))
    spread = lax.all_to_all(context, "ctx", 0, 0, tiled=True).reshape(width, tok_rows)
    mixed = jnp.einsum("ft,fo->to", spread, out_full, preferred_element_type=jnp.float32)
    mixed = mixed + out_shift
    return (current.astype(jnp.float32) + layer_scale * mixed).astype(jnp.bfloat16)


def ring_gather(piece, axis, on_block):
    count = lax.axis_size(axis)
    right = [(i, (i + 1) % count) for i in range(count)]
    left = [(i, (i - 1) % count) for i in range(count)]
    blocks = [None] * count
    made = [None] * count
    blocks[0], made[0] = piece, on_block(piece)
    forward, backward = piece, piece
    for step in range(count // 2):
        forward = lax.ppermute(forward, axis, right)
        k = count - 1 - step
        blocks[k], made[k] = forward, on_block(forward)
        if step < (count - 1) // 2:
            backward = lax.ppermute(backward, axis, left)
            k = 1 + step
            blocks[k], made[k] = backward, on_block(backward)
    return jnp.concatenate(blocks, axis=1), jnp.concatenate(made, axis=1)


def unrotate(rotated, axis):
    count = lax.axis_size(axis)
    cols = rotated.shape[1]
    shift = lax.axis_index(axis) * (cols // count)
    doubled = jnp.concatenate([rotated, rotated], axis=1)
    return lax.dynamic_slice_in_dim(doubled, cols - shift, cols, axis=1)


def per_device(patches, lengths, norm_gain, norm_bias, w_qkv, w_out, out_bias, scale_gain):
    section_index = lax.axis_index("pipe")
    section_count = lax.axis_size("pipe")
    core = lax.axis_index("ctx") % 2
    width = w_qkv.shape[1]
    half = width // 2
    rows_mine = lax.dynamic_slice_in_dim(w_qkv[0], core * half, half, axis=0)
    sibling = [(i, i ^ 1) for i in range(lax.axis_size("ctx"))]
    current = patches[0, 0]
    normed = normalize(current, norm_gain[0], norm_bias[0])
    both = jnp.concatenate([normed, lax.ppermute(normed, "ctx", sibling)], axis=0)
    both = lax.dynamic_slice_in_dim(both, core * half, half, axis=1)
    qkv_mine, partial = ring_gather(
        rows_mine, "dp", lambda block: jnp.dot(both, block, preferred_element_type=jnp.float32)
    )
    tok_rows = current.shape[0]
    partial_other = lax.ppermute(partial[tok_rows:], "ctx", sibling)
    first = unrotate((partial[:tok_rows] + partial_other).astype(jnp.bfloat16), "dp")
    qkv_other = lax.ppermute(qkv_mine, "ctx", sibling)
    args = (qkv_mine, qkv_other, w_out[0], norm_gain[0], norm_bias[0], out_bias[0], scale_gain[0])
    length = lengths[0, 0]
    outputs = []
    for turn_index in range(section_count):
        produced = sublayer(current, length, *args, projected=first if turn_index == 0 else None)
        outputs.append(produced)
        if turn_index + 1 < section_count:
            pairs = [(i, i + 1) for i in range(section_count - 1)]
            current = lax.ppermute(produced, "pipe", pairs)
    result = outputs[0]
    for turn_index in range(1, section_count):
        result = jnp.where(section_index == turn_index, outputs[turn_index], result)
    return result[None, None, None]


def solution(mesh):
    in_specs = (
        P(None, "dp", "ctx", None),
        P(None, "dp"),
        P("pipe", None),
        P("pipe", None),
        P("pipe", None, "dp"),
        P("pipe", None, None),
        P("pipe", None),
        P("pipe", None),
    )
    out_specs = P("pipe", None, "dp", "ctx", None)
    return jax.shard_map(
        per_device, mesh=mesh, in_specs=in_specs, out_specs=out_specs, check_vma=False
    )
```

```python
import jax
import jax.numpy as jnp
from jax import lax
from jax.sharding import PartitionSpec as P

HEADS = 16


epsilon = 1e-06
masked_score = -1e30


def normalize(hidden, gain, shift):
    values = hidden.astype(jnp.float32)
    row_mean = jnp.mean(values, axis=-1, keepdims=True)
    centered = values - row_mean
    variance = jnp.mean(centered * centered, axis=-1, keepdims=True)
    return (centered * lax.rsqrt(variance + epsilon) * gain + shift).astype(jnp.bfloat16)


def head_attention(qkv, length, score_scale):
    queries, key_rows, value_rows = qkv[0], qkv[1], qkv[2]
    count = qkv.shape[-1]
    scores = (
        jnp.einsum("dq,dk->qk", queries, key_rows, preferred_element_type=jnp.float32)
        * score_scale
    )
    valid = jnp.arange(count, dtype=jnp.int32) < length
    top = jnp.max(jnp.where(valid[None, :], scores, masked_score), axis=-1)
    weights = jnp.where(valid[None, :], jnp.exp(scores - top[:, None]), 0.0)
    totals = jnp.sum(weights, axis=-1)
    context = jnp.einsum(
        "qk,dk->dq", weights.astype(jnp.bfloat16), value_rows, preferred_element_type=jnp.float32
    )
    return (context / totals[None, :]).astype(jnp.bfloat16)


def sublayer(current, length, qkv_mine, qkv_other, out_full, gain, shift, out_shift, layer_scale,
             projected=None, to_both=False):
    tok_rows, width = current.shape
    head_width = width // HEADS
    ctx_count = lax.axis_size("ctx")
    core = lax.axis_index("ctx") % 2
    half = width // 2
    if projected is None:
        normed = normalize(current, gain, shift)
        normed_mine = lax.dynamic_slice_in_dim(normed, core * half, half, axis=1)
        normed_other = lax.dynamic_slice_in_dim(normed, (1 - core) * half, half, axis=1)
        projected = jnp.dot(normed_mine, qkv_mine, preferred_element_type=jnp.float32) + jnp.dot(
            normed_other, qkv_other, preferred_element_type=jnp.float32
        )
        projected = unrotate(projected.astype(jnp.bfloat16), "dp")
    projected = jnp.transpose(projected.reshape(tok_rows, 3, HEADS, head_width), (2, 1, 3, 0))
    gathered = lax.all_to_all(projected, "ctx", 0, 3, tiled=True)
    context = head_attention(gathered[0], length, head_width ** (-0.5))
    context = jnp.transpose(context.reshape(head_width, ctx_count, tok_rows), (1, 0, 2))
    if to_both:
        sent = jnp.concatenate([context] * lax.axis_size("pipe"), axis=0)
        spread = lax.all_to_all(sent, ("pipe", "ctx"), 0, 0, tiled=True)[:ctx_count]
    else:
        spread = lax.all_to_all(context, "ctx", 0, 0, tiled=True)
    spread = spread.reshape(width, tok_rows)
    mixed = jnp.einsum("ft,fo->to", spread, out_full, preferred_element_type=jnp.float32)
    mixed = mixed + out_shift
    return (current.astype(jnp.float32) + layer_scale * mixed).astype(jnp.bfloat16)


def ring_gather(piece, axis, on_block):
    count = lax.axis_size(axis)
    right = [(i, (i + 1) % count) for i in range(count)]
    left = [(i, (i - 1) % count) for i in range(count)]
    blocks = [None] * count
    made = [None] * count
    blocks[0], made[0] = piece, on_block(piece)
    forward, backward = piece, piece
    for step in range(count // 2):
        forward = lax.ppermute(forward, axis, right)
        k = count - 1 - step
        blocks[k], made[k] = forward, on_block(forward)
        if step < (count - 1) // 2:
            backward = lax.ppermute(backward, axis, left)
            k = 1 + step
            blocks[k], made[k] = backward, on_block(backward)
    return jnp.concatenate(blocks, axis=1), jnp.concatenate(made, axis=1)


def unrotate(rotated, axis):
    count = lax.axis_size(axis)
    cols = rotated.shape[1]
    shift = lax.axis_index(axis) * (cols // count)
    doubled = jnp.concatenate([rotated, rotated], axis=1)
    return lax.dynamic_slice_in_dim(doubled, cols - shift, cols, axis=1)


def per_device(patches, lengths, norm_gain, norm_bias, w_qkv, w_out, out_bias, scale_gain):
    section_index = lax.axis_index("pipe")
    section_count = lax.axis_size("pipe")
    core = lax.axis_index("ctx") % 2
    width = w_qkv.shape[1]
    half = width // 2
    rows_mine = lax.dynamic_slice_in_dim(w_qkv[0], core * half, half, axis=0)
    sibling = [(i, i ^ 1) for i in range(lax.axis_size("ctx"))]
    current = patches[0, 0]
    normed = normalize(current, norm_gain[0], norm_bias[0])
    both = jnp.concatenate([normed, lax.ppermute(normed, "ctx", sibling)], axis=0)
    both = lax.dynamic_slice_in_dim(both, core * half, half, axis=1)
    qkv_mine, partial = ring_gather(
        rows_mine, "dp", lambda block: jnp.dot(both, block, preferred_element_type=jnp.float32)
    )
    tok_rows = current.shape[0]
    partial_other = lax.ppermute(partial[tok_rows:], "ctx", sibling)
    first = unrotate((partial[:tok_rows] + partial_other).astype(jnp.bfloat16), "dp")
    qkv_other = lax.ppermute(qkv_mine, "ctx", sibling)
    args = (qkv_mine, qkv_other, w_out[0], norm_gain[0], norm_bias[0], out_bias[0], scale_gain[0])
    length = lengths[0, 0]
    first_params = (w_out[0], out_bias[0], scale_gain[0])
    onward = [(i, j) for i in range(1) for j in range(1, section_count)]
    first_params = tuple(
        jnp.where(section_index == 0, own, lax.ppermute(own, "pipe", onward))
        for own in first_params
    )
    turn0_args = (qkv_mine, qkv_other, first_params[0], norm_gain[0], norm_bias[0],
                  first_params[1], first_params[2])
    assert section_count == 2
    produced = sublayer(current, length, *turn0_args, projected=first, to_both=True)
    outputs = [produced, sublayer(produced, length, *args)]
    result = outputs[0]
    for turn_index in range(1, section_count):
        result = jnp.where(section_index == turn_index, outputs[turn_index], result)
    return result[None, None, None]


def solution(mesh):
    in_specs = (
        P(None, "dp", "ctx", None),
        P(None, "dp"),
        P("pipe", None),
        P("pipe", None),
        P("pipe", None, "dp"),
        P("pipe", None, None),
        P("pipe", None),
        P("pipe", None),
    )
    out_specs = P("pipe", None, "dp", "ctx", None)
    return jax.shard_map(
        per_device, mesh=mesh, in_specs=in_specs, out_specs=out_specs, check_vma=False
    )
```

```python
import jax
import jax.numpy as jnp
from jax import lax
from jax.experimental import pallas as pl
from jax.experimental.pallas import tpu as pltpu
from jax.sharding import PartitionSpec as P

HEADS = 16


epsilon = 1e-06
masked_score = -1e30


def normalize(hidden, gain, shift):
    values = hidden.astype(jnp.float32)
    row_mean = jnp.mean(values, axis=-1, keepdims=True)
    centered = values - row_mean
    variance = jnp.mean(centered * centered, axis=-1, keepdims=True)
    return (centered * lax.rsqrt(variance + epsilon) * gain + shift).astype(jnp.bfloat16)


def attention_kernel(score_scale, length_ref, qkv_ref, out_ref):
    block = out_ref.shape[1]
    start = pl.multiple_of(pl.program_id(0) * block, block)
    queries = qkv_ref[0, :, pl.ds(start, block)]
    key_rows = qkv_ref[1]
    value_rows = qkv_ref[2]
    scores = lax.dot_general(
        key_rows, queries, (((0,), (0,)), ((), ())), preferred_element_type=jnp.float32
    ) * score_scale
    valid = lax.broadcasted_iota(jnp.int32, scores.shape, 0) < length_ref[0]
    top = jnp.max(jnp.where(valid, scores, masked_score), axis=0, keepdims=True)
    weights = jnp.where(valid, jnp.exp(scores - top), 0.0)
    totals = jnp.sum(weights, axis=0, keepdims=True)
    context = jnp.dot(value_rows, weights.astype(jnp.bfloat16), preferred_element_type=jnp.float32)
    out_ref[...] = (context / totals).astype(out_ref.dtype)


def head_attention(qkv, length, score_scale):
    _, head_width, count = qkv.shape
    block = 256
    return pl.pallas_call(
        lambda *refs: attention_kernel(score_scale, *refs),
        out_shape=jax.ShapeDtypeStruct((head_width, count), jnp.bfloat16),
        grid_spec=pltpu.PrefetchScalarGridSpec(
            num_scalar_prefetch=1,
            grid=(count // block,),
            in_specs=[pl.BlockSpec(qkv.shape, lambda i, n: (0, 0, 0))],
            out_specs=pl.BlockSpec((head_width, block), lambda i, n: (0, i)),
        ),
        cost_estimate=pl.CostEstimate(
            flops=4 * count * count * head_width,
            transcendentals=count * count,
            bytes_accessed=4 * head_width * count * 2,
        ),
    )(jnp.reshape(length, (1,)).astype(jnp.int32), qkv)


def sublayer(current, length, qkv_mine, qkv_other, out_full, gain, shift, out_shift, layer_scale,
             projected=None):
    tok_rows, width = current.shape
    head_width = width // HEADS
    ctx_count = lax.axis_size("ctx")
    core = lax.axis_index("ctx") % 2
    half = width // 2
    if projected is None:
        normed = normalize(current, gain, shift)
        normed_mine = lax.dynamic_slice_in_dim(normed, core * half, half, axis=1)
        normed_other = lax.dynamic_slice_in_dim(normed, (1 - core) * half, half, axis=1)
        projected = jnp.dot(normed_mine, qkv_mine, preferred_element_type=jnp.float32) + jnp.dot(
            normed_other, qkv_other, preferred_element_type=jnp.float32
        )
        projected = unrotate(projected.astype(jnp.bfloat16), "dp")
    projected = jnp.transpose(projected.reshape(tok_rows, 3, HEADS, head_width), (2, 1, 3, 0))
    gathered = lax.all_to_all(projected, "ctx", 0, 3, tiled=True)
    context = head_attention(gathered[0], length, head_width ** (-0.5))
    context = jnp.transpose(context.reshape(head_width, ctx_count, tok_rows), (1, 0, 2))
    spread = lax.all_to_all(context, "ctx", 0, 0, tiled=True).reshape(width, tok_rows)
    mixed = jnp.einsum("ft,fo->to", spread, out_full, preferred_element_type=jnp.float32)
    mixed = mixed + out_shift
    return (current.astype(jnp.float32) + layer_scale * mixed).astype(jnp.bfloat16)


def ring_gather(piece, axis, on_block):
    count = lax.axis_size(axis)
    right = [(i, (i + 1) % count) for i in range(count)]
    left = [(i, (i - 1) % count) for i in range(count)]
    blocks = [None] * count
    made = [None] * count
    blocks[0], made[0] = piece, on_block(piece)
    forward, backward = piece, piece
    for step in range(count // 2):
        forward = lax.ppermute(forward, axis, right)
        k = count - 1 - step
        blocks[k], made[k] = forward, on_block(forward)
        if step < (count - 1) // 2:
            backward = lax.ppermute(backward, axis, left)
            k = 1 + step
            blocks[k], made[k] = backward, on_block(backward)
    return jnp.concatenate(blocks, axis=1), jnp.concatenate(made, axis=1)


def unrotate(rotated, axis):
    count = lax.axis_size(axis)
    cols = rotated.shape[1]
    shift = lax.axis_index(axis) * (cols // count)
    doubled = jnp.concatenate([rotated, rotated], axis=1)
    return lax.dynamic_slice_in_dim(doubled, cols - shift, cols, axis=1)


def per_device(patches, lengths, norm_gain, norm_bias, w_qkv, w_out, out_bias, scale_gain):
    section_index = lax.axis_index("pipe")
    section_count = lax.axis_size("pipe")
    core = lax.axis_index("ctx") % 2
    width = w_qkv.shape[1]
    half = width // 2
    rows_mine = lax.dynamic_slice_in_dim(w_qkv[0], core * half, half, axis=0)
    sibling = [(i, i ^ 1) for i in range(lax.axis_size("ctx"))]
    current = patches[0, 0]
    normed = normalize(current, norm_gain[0], norm_bias[0])
    both = jnp.concatenate([normed, lax.ppermute(normed, "ctx", sibling)], axis=0)
    both = lax.dynamic_slice_in_dim(both, core * half, half, axis=1)
    qkv_mine, partial = ring_gather(
        rows_mine, "dp", lambda block: jnp.dot(both, block, preferred_element_type=jnp.float32)
    )
    tok_rows = current.shape[0]
    partial_other = lax.ppermute(partial[tok_rows:], "ctx", sibling)
    first = unrotate((partial[:tok_rows] + partial_other).astype(jnp.bfloat16), "dp")
    qkv_other = lax.ppermute(qkv_mine, "ctx", sibling)
    args = (qkv_mine, qkv_other, w_out[0], norm_gain[0], norm_bias[0], out_bias[0], scale_gain[0])
    length = lengths[0, 0]
    outputs = []
    for turn_index in range(section_count):
        produced = sublayer(current, length, *args, projected=first if turn_index == 0 else None)
        outputs.append(produced)
        if turn_index + 1 < section_count:
            pairs = [(i, i + 1) for i in range(section_count - 1)]
            current = lax.ppermute(produced, "pipe", pairs)
    result = outputs[0]
    for turn_index in range(1, section_count):
        result = jnp.where(section_index == turn_index, outputs[turn_index], result)
    return result[None, None, None]


def solution(mesh):
    in_specs = (
        P(None, "dp", "ctx", None),
        P(None, "dp"),
        P("pipe", None),
        P("pipe", None),
        P("pipe", None, "dp"),
        P("pipe", None, None),
        P("pipe", None),
        P("pipe", None),
    )
    out_specs = P("pipe", None, "dp", "ctx", None)
    return jax.shard_map(
        per_device, mesh=mesh, in_specs=in_specs, out_specs=out_specs, check_vma=False
    )
```

```python
import jax
import jax.numpy as jnp
from jax import lax
from jax.sharding import PartitionSpec as P

HEADS = 16


epsilon = 1e-06
masked_score = -1e30


def normalize(hidden, gain, shift):
    values = hidden.astype(jnp.float32)
    row_mean = jnp.mean(values, axis=-1, keepdims=True)
    centered = values - row_mean
    variance = jnp.mean(centered * centered, axis=-1, keepdims=True)
    return (centered * lax.rsqrt(variance + epsilon) * gain + shift).astype(jnp.bfloat16)


def head_attention(qkv, length, score_scale):
    queries, key_rows, value_rows = qkv[0], qkv[1], qkv[2]
    count = qkv.shape[-1]
    scores = (
        jnp.einsum("dq,dk->qk", queries, key_rows, preferred_element_type=jnp.float32)
        * score_scale
    )
    valid = jnp.arange(count, dtype=jnp.int32) < length
    top = jnp.max(jnp.where(valid[None, :], scores, masked_score), axis=-1)
    weights = jnp.where(valid[None, :], jnp.exp(scores - top[:, None]), 0.0)
    totals = jnp.sum(weights, axis=-1)
    context = jnp.einsum(
        "qk,dk->dq", weights.astype(jnp.bfloat16), value_rows, preferred_element_type=jnp.float32
    )
    return (context / totals[None, :]).astype(jnp.bfloat16)


def sublayer(current, length, qkv_mine, qkv_other, out_full, gain, shift, out_shift, layer_scale,
             projected=None):
    tok_rows, width = current.shape
    head_width = width // HEADS
    ctx_count = lax.axis_size("ctx")
    core = lax.axis_index("ctx") % 2
    half = width // 2
    if projected is None:
        normed = normalize(current, gain, shift)
        normed_mine = lax.dynamic_slice_in_dim(normed, core * half, half, axis=1)
        normed_other = lax.dynamic_slice_in_dim(normed, (1 - core) * half, half, axis=1)
        projected = jnp.dot(normed_mine, qkv_mine, preferred_element_type=jnp.float32) + jnp.dot(
            normed_other, qkv_other, preferred_element_type=jnp.float32
        )
        projected = unrotate(projected.astype(jnp.bfloat16), "dp")
        projected = jnp.transpose(
            projected.reshape(tok_rows, 3, HEADS, head_width), (2, 1, 3, 0)
        )
    gathered = lax.all_to_all(projected, "ctx", 0, 3, tiled=True)
    context = head_attention(gathered[0], length, head_width ** (-0.5))
    context = jnp.transpose(context.reshape(head_width, ctx_count, tok_rows), (1, 0, 2))
    spread = lax.all_to_all(context, "ctx", 0, 0, tiled=True).reshape(width, tok_rows)
    mixed = jnp.einsum("ft,fo->to", spread, out_full, preferred_element_type=jnp.float32)
    mixed = mixed + out_shift
    return (current.astype(jnp.float32) + layer_scale * mixed).astype(jnp.bfloat16)


def ring_gather(piece, axis, on_block, made_axis=1):
    count = lax.axis_size(axis)
    right = [(i, (i + 1) % count) for i in range(count)]
    left = [(i, (i - 1) % count) for i in range(count)]
    blocks = [None] * count
    made = [None] * count
    blocks[0], made[0] = piece, on_block(piece)
    forward, backward = piece, piece
    for step in range(count // 2):
        forward = lax.ppermute(forward, axis, right)
        k = count - 1 - step
        blocks[k], made[k] = forward, on_block(forward)
        if step < (count - 1) // 2:
            backward = lax.ppermute(backward, axis, left)
            k = 1 + step
            blocks[k], made[k] = backward, on_block(backward)
    return jnp.concatenate(blocks, axis=1), jnp.concatenate(made, axis=made_axis)


def unrotate(rotated, axis, along=1):
    count = lax.axis_size(axis)
    cols = rotated.shape[along]
    shift = lax.axis_index(axis) * (cols // count)
    doubled = jnp.concatenate([rotated, rotated], axis=along)
    return lax.dynamic_slice_in_dim(doubled, cols - shift, cols, axis=along)


def per_device(patches, lengths, norm_gain, norm_bias, w_qkv, w_out, out_bias, scale_gain):
    section_index = lax.axis_index("pipe")
    section_count = lax.axis_size("pipe")
    core = lax.axis_index("ctx") % 2
    width = w_qkv.shape[1]
    half = width // 2
    rows_mine = lax.dynamic_slice_in_dim(w_qkv[0], core * half, half, axis=0)
    sibling = [(i, i ^ 1) for i in range(lax.axis_size("ctx"))]
    current = patches[0, 0]
    normed = normalize(current, norm_gain[0], norm_bias[0])
    normed_sibling = lax.ppermute(normed, "ctx", sibling)
    mine_rows = lax.dynamic_slice_in_dim(normed, core * half, half, axis=1)
    sibling_rows = lax.dynamic_slice_in_dim(normed_sibling, core * half, half, axis=1)

    both = jnp.stack([mine_rows, sibling_rows])

    def on_block(block):
        return jnp.einsum("kc,stk->sct", block, both, preferred_element_type=jnp.float32)

    qkv_mine, partial = ring_gather(rows_mine, "dp", on_block, made_axis=1)
    tok_rows = current.shape[0]
    partial_other = lax.ppermute(partial[1], "ctx", sibling)
    first = unrotate((partial[0] + partial_other).astype(jnp.bfloat16), "dp", along=0)
    first = jnp.transpose(first.reshape(3, HEADS, width // HEADS, tok_rows), (1, 0, 2, 3))
    qkv_other = lax.ppermute(qkv_mine, "ctx", sibling)
    args = (qkv_mine, qkv_other, w_out[0], norm_gain[0], norm_bias[0], out_bias[0], scale_gain[0])
    length = lengths[0, 0]
    outputs = []
    for turn_index in range(section_count):
        produced = sublayer(current, length, *args, projected=first if turn_index == 0 else None)
        outputs.append(produced)
        if turn_index + 1 < section_count:
            pairs = [(i, i + 1) for i in range(section_count - 1)]
            current = lax.ppermute(produced, "pipe", pairs)
    result = outputs[0]
    for turn_index in range(1, section_count):
        result = jnp.where(section_index == turn_index, outputs[turn_index], result)
    return result[None, None, None]


def solution(mesh):
    in_specs = (
        P(None, "dp", "ctx", None),
        P(None, "dp"),
        P("pipe", None),
        P("pipe", None),
        P("pipe", None, "dp"),
        P("pipe", None, None),
        P("pipe", None),
        P("pipe", None),
    )
    out_specs = P("pipe", None, "dp", "ctx", None)
    return jax.shard_map(
        per_device, mesh=mesh, in_specs=in_specs, out_specs=out_specs, check_vma=False
    )
```

```python
import jax
import jax.numpy as jnp
from jax import lax
from jax.sharding import PartitionSpec as P

HEADS = 16


epsilon = 1e-06
masked_score = -1e30


def normalize(hidden, gain, shift):
    values = hidden.astype(jnp.float32)
    row_mean = jnp.mean(values, axis=-1, keepdims=True)
    centered = values - row_mean
    variance = jnp.mean(centered * centered, axis=-1, keepdims=True)
    return (centered * lax.rsqrt(variance + epsilon) * gain + shift).astype(jnp.bfloat16)


def head_attention(qkv, length, score_scale):
    queries, key_rows, value_rows = qkv[0], qkv[1], qkv[2]
    count = qkv.shape[-1]
    scores = (
        jnp.einsum("dq,dk->qk", queries, key_rows, preferred_element_type=jnp.float32)
        * score_scale
    )
    valid = jnp.arange(count, dtype=jnp.int32) < length
    top = jnp.max(jnp.where(valid[None, :], scores, masked_score), axis=-1)
    weights = jnp.where(valid[None, :], jnp.exp(scores - top[:, None]), 0.0)
    totals = jnp.sum(weights, axis=-1)
    context = jnp.einsum(
        "qk,dk->dq", weights.astype(jnp.bfloat16), value_rows, preferred_element_type=jnp.float32
    )
    return (context / totals[None, :]).astype(jnp.bfloat16)


def sublayer(current, length, qkv_mine, qkv_other, out_full, gain, shift, out_shift, layer_scale,
             projected=None):
    tok_rows, width = current.shape
    head_width = width // HEADS
    ctx_count = lax.axis_size("ctx")
    core = lax.axis_index("ctx") % 2
    half = width // 2
    if projected is None:
        normed = normalize(current, gain, shift)
        normed_mine = lax.dynamic_slice_in_dim(normed, core * half, half, axis=1)
        normed_other = lax.dynamic_slice_in_dim(normed, (1 - core) * half, half, axis=1)
        projected = jnp.dot(normed_mine, qkv_mine, preferred_element_type=jnp.float32) + jnp.dot(
            normed_other, qkv_other, preferred_element_type=jnp.float32
        )
        projected = unrotate(projected.astype(jnp.bfloat16), "dp")
        projected = jnp.transpose(
            projected.reshape(tok_rows, 3, HEADS, head_width), (2, 1, 3, 0)
        )
    gathered = lax.all_to_all(projected, "ctx", 0, 3, tiled=True)
    context = head_attention(gathered[0], length, head_width ** (-0.5))
    context = jnp.transpose(context.reshape(head_width, ctx_count, tok_rows), (1, 0, 2))
    spread = lax.all_to_all(context, "ctx", 0, 0, tiled=True).reshape(width, tok_rows)
    mixed = jnp.einsum("ft,fo->to", spread, out_full, preferred_element_type=jnp.float32)
    mixed = mixed + out_shift
    return (current.astype(jnp.float32) + layer_scale * mixed).astype(jnp.bfloat16)


def ring_gather(piece, axis, on_block, made_axis):
    count = lax.axis_size(axis)
    right = [(i, (i + 1) % count) for i in range(count)]
    left = [(i, (i - 1) % count) for i in range(count)]
    blocks = [None] * count
    made = [None] * count
    blocks[0], made[0] = piece, on_block(piece)
    forward, backward = piece, piece
    for step in range(count // 2):
        forward = lax.ppermute(forward, axis, right)
        k = count - 1 - step
        blocks[k], made[k] = forward, on_block(forward)
        if step < (count - 1) // 2:
            backward = lax.ppermute(backward, axis, left)
            k = 1 + step
            blocks[k], made[k] = backward, on_block(backward)
    blocks = lax.optimization_barrier(blocks)
    made = [jnp.concatenate(parts, axis=made_axis) for parts in zip(*made)]
    return jnp.concatenate(blocks, axis=1), made


def unrotate(rotated, axis, along=1):
    count = lax.axis_size(axis)
    cols = rotated.shape[along]
    shift = lax.axis_index(axis) * (cols // count)
    doubled = jnp.concatenate([rotated, rotated], axis=along)
    return lax.dynamic_slice_in_dim(doubled, cols - shift, cols, axis=along)


def per_device(patches, lengths, norm_gain, norm_bias, w_qkv, w_out, out_bias, scale_gain):
    section_index = lax.axis_index("pipe")
    section_count = lax.axis_size("pipe")
    core = lax.axis_index("ctx") % 2
    width = w_qkv.shape[1]
    half = width // 2
    rows_mine = lax.dynamic_slice_in_dim(w_qkv[0], core * half, half, axis=0)
    sibling = [(i, i ^ 1) for i in range(lax.axis_size("ctx"))]
    current = patches[0, 0]
    normed = normalize(current, norm_gain[0], norm_bias[0])
    normed_sibling = lax.ppermute(normed, "ctx", sibling)
    mine_rows = lax.dynamic_slice_in_dim(normed, core * half, half, axis=1)
    sibling_rows = lax.dynamic_slice_in_dim(normed_sibling, core * half, half, axis=1)

    def on_block(block):
        return tuple(
            jnp.einsum("kc,tk->ct", block, rows, preferred_element_type=jnp.float32)
            for rows in (mine_rows, sibling_rows)
        )

    qkv_mine, partial = ring_gather(rows_mine, "dp", on_block, made_axis=0)
    tok_rows = current.shape[0]
    partial_other = lax.ppermute(partial[1], "ctx", sibling)
    first = unrotate((partial[0] + partial_other).astype(jnp.bfloat16), "dp", along=0)
    first = jnp.transpose(first.reshape(3, HEADS, width // HEADS, tok_rows), (1, 0, 2, 3))
    qkv_other = lax.ppermute(qkv_mine, "ctx", sibling)
    args = (qkv_mine, qkv_other, w_out[0], norm_gain[0], norm_bias[0], out_bias[0], scale_gain[0])
    length = lengths[0, 0]
    outputs = []
    for turn_index in range(section_count):
        produced = sublayer(current, length, *args, projected=first if turn_index == 0 else None)
        outputs.append(produced)
        if turn_index + 1 < section_count:
            pairs = [(i, i + 1) for i in range(section_count - 1)]
            current = lax.ppermute(produced, "pipe", pairs)
    result = outputs[0]
    for turn_index in range(1, section_count):
        result = jnp.where(section_index == turn_index, outputs[turn_index], result)
    return result[None, None, None]


def solution(mesh):
    in_specs = (
        P(None, "dp", "ctx", None),
        P(None, "dp"),
        P("pipe", None),
        P("pipe", None),
        P("pipe", None, "dp"),
        P("pipe", None, None),
        P("pipe", None),
        P("pipe", None),
    )
    out_specs = P("pipe", None, "dp", "ctx", None)
    return jax.shard_map(
        per_device, mesh=mesh, in_specs=in_specs, out_specs=out_specs, check_vma=False
    )
```

```python
import jax
import numpy as np
import jax.numpy as jnp
from jax import lax
from jax.sharding import PartitionSpec as P

HEADS = 16


epsilon = 1e-06
masked_score = -1e30


def normalize(hidden, gain, shift):
    values = hidden.astype(jnp.float32)
    row_mean = jnp.mean(values, axis=-1, keepdims=True)
    centered = values - row_mean
    variance = jnp.mean(centered * centered, axis=-1, keepdims=True)
    return (centered * lax.rsqrt(variance + epsilon) * gain + shift).astype(jnp.bfloat16)


def head_attention(qkv, length, score_scale, positions):
    queries, key_rows, value_rows = qkv[0], qkv[1], qkv[2]
    count = qkv.shape[-1]
    scores = (
        jnp.einsum("dq,dk->qk", queries, key_rows, preferred_element_type=jnp.float32)
        * score_scale
    )
    valid = positions < length
    top = jnp.max(jnp.where(valid[None, :], scores, masked_score), axis=-1)
    weights = jnp.where(valid[None, :], jnp.exp(scores - top[:, None]), 0.0)
    totals = jnp.sum(weights, axis=-1)
    context = jnp.einsum(
        "qk,dk->dq", weights.astype(jnp.bfloat16), value_rows, preferred_element_type=jnp.float32
    )
    return (context / totals[None, :]).astype(jnp.bfloat16)


def sublayer(current, length, qkv_mine, qkv_other, out_full, gain, shift, out_shift, layer_scale,
             projected=None, chunk_of=None, residual=None):
    tok_rows, width = current.shape
    head_width = width // HEADS
    ctx_count = lax.axis_size("ctx")
    core = lax.axis_index("ctx") % 2
    half = width // 2
    if projected is None:
        normed = normalize(current, gain, shift)
        normed_mine = lax.dynamic_slice_in_dim(normed, core * half, half, axis=1)
        normed_other = lax.dynamic_slice_in_dim(normed, (1 - core) * half, half, axis=1)
        projected = jnp.dot(normed_mine, qkv_mine, preferred_element_type=jnp.float32) + jnp.dot(
            normed_other, qkv_other, preferred_element_type=jnp.float32
        )
        projected = unrotate(projected.astype(jnp.bfloat16), "dp")
        projected = jnp.transpose(
            projected.reshape(tok_rows, 3, HEADS, head_width), (2, 1, 3, 0)
        )
    gathered = lax.all_to_all(projected, "ctx", 0, 3, tiled=True)
    chunk_of = list(range(ctx_count)) if chunk_of is None else chunk_of
    positions = np.arange(ctx_count * tok_rows).reshape(ctx_count, tok_rows)[chunk_of]
    context = head_attention(
        gathered[0], length, head_width ** (-0.5), jnp.asarray(positions.reshape(-1), jnp.int32)
    )
    context = jnp.transpose(context.reshape(head_width, ctx_count, tok_rows), (1, 0, 2))
    if chunk_of != list(range(ctx_count)):
        held_at = [chunk_of.index(t) for t in range(ctx_count)]
        context = jnp.concatenate([context[k : k + 1] for k in held_at], axis=0)
    spread = lax.all_to_all(context, "ctx", 0, 0, tiled=True).reshape(width, tok_rows)
    mixed = jnp.einsum("ft,fo->to", spread, out_full, preferred_element_type=jnp.float32)
    mixed = mixed + out_shift
    residual = current if residual is None else residual
    return (residual.astype(jnp.float32) + layer_scale * mixed).astype(jnp.bfloat16)


def ring_gather(piece, axis, on_block, made_axis=1):
    count = lax.axis_size(axis)
    right = [(i, (i + 1) % count) for i in range(count)]
    left = [(i, (i - 1) % count) for i in range(count)]
    blocks = [None] * count
    made = [None] * count
    blocks[0], made[0] = piece, on_block(piece)
    forward, backward = piece, piece
    for step in range(count // 2):
        forward = lax.ppermute(forward, axis, right)
        k = count - 1 - step
        blocks[k], made[k] = forward, on_block(forward)
        if step < (count - 1) // 2:
            backward = lax.ppermute(backward, axis, left)
            k = 1 + step
            blocks[k], made[k] = backward, on_block(backward)
    return jnp.concatenate(blocks, axis=1), jnp.concatenate(made, axis=made_axis)


def unrotate(rotated, axis, along=1):
    count = lax.axis_size(axis)
    cols = rotated.shape[along]
    shift = lax.axis_index(axis) * (cols // count)
    doubled = jnp.concatenate([rotated, rotated], axis=along)
    return lax.dynamic_slice_in_dim(doubled, cols - shift, cols, axis=along)


def per_device(patches, lengths, norm_gain, norm_bias, w_qkv, w_out, out_bias, scale_gain):
    section_index = lax.axis_index("pipe")
    section_count = lax.axis_size("pipe")
    core = lax.axis_index("ctx") % 2
    width = w_qkv.shape[1]
    half = width // 2
    rows_mine = lax.dynamic_slice_in_dim(w_qkv[0], core * half, half, axis=0)
    sibling = [(i, i ^ 1) for i in range(lax.axis_size("ctx"))]
    current = patches[0, 0]
    normed = normalize(current, norm_gain[0], norm_bias[0])
    normed_sibling = lax.ppermute(normed, "ctx", sibling)
    mine_rows = lax.dynamic_slice_in_dim(normed, core * half, half, axis=1)
    sibling_rows = lax.dynamic_slice_in_dim(normed_sibling, core * half, half, axis=1)

    both = jnp.stack([mine_rows, sibling_rows])

    def on_block(block):
        return jnp.einsum("kc,stk->sct", block, both, preferred_element_type=jnp.float32)

    qkv_mine, partial = ring_gather(rows_mine, "dp", on_block, made_axis=1)
    tok_rows = current.shape[0]
    partial_other = lax.ppermute(partial[1], "ctx", sibling)
    first = unrotate((partial[0] + partial_other).astype(jnp.bfloat16), "dp", along=0)
    first = jnp.transpose(first.reshape(3, HEADS, width // HEADS, tok_rows), (1, 0, 2, 3))
    qkv_other = lax.ppermute(qkv_mine, "ctx", sibling)
    args = (qkv_mine, qkv_other, w_out[0], norm_gain[0], norm_bias[0], out_bias[0], scale_gain[0])
    length = lengths[0, 0]
    assert section_count == 2
    ctx_count = lax.axis_size("ctx")
    produced = sublayer(current, length, *args, projected=first)
    flip = 2
    onward = [(c, ctx_count + (c ^ flip)) for c in range(ctx_count)]
    handed = lax.ppermute(produced, ("pipe", "ctx"), onward)
    residual = lax.ppermute(handed, "ctx", [(c, c ^ flip) for c in range(ctx_count)])
    chunk_of = [c ^ flip for c in range(ctx_count)]
    outputs = [produced, sublayer(handed, length, *args, chunk_of=chunk_of, residual=residual)]
    result = outputs[0]
    for turn_index in range(1, section_count):
        result = jnp.where(section_index == turn_index, outputs[turn_index], result)
    return result[None, None, None]


def solution(mesh):
    in_specs = (
        P(None, "dp", "ctx", None),
        P(None, "dp"),
        P("pipe", None),
        P("pipe", None),
        P("pipe", None, "dp"),
        P("pipe", None, None),
        P("pipe", None),
        P("pipe", None),
    )
    out_specs = P("pipe", None, "dp", "ctx", None)
    return jax.shard_map(
        per_device, mesh=mesh, in_specs=in_specs, out_specs=out_specs, check_vma=False
    )
```

```python
import jax
import jax.numpy as jnp
from jax import lax
from jax.sharding import PartitionSpec as P

HEADS = 16


epsilon = 1e-06
masked_score = -1e30


def normalize(hidden, gain, shift):
    values = hidden.astype(jnp.float32)
    row_mean = jnp.mean(values, axis=-1, keepdims=True)
    centered = values - row_mean
    variance = jnp.mean(centered * centered, axis=-1, keepdims=True)
    return (centered * lax.rsqrt(variance + epsilon) * gain + shift).astype(jnp.bfloat16)


def head_attention(qkv, length, score_scale):
    queries, key_rows, value_rows = qkv[0], qkv[1], qkv[2]
    count = qkv.shape[-1]
    scores = (
        jnp.einsum("dq,dk->qk", queries, key_rows, preferred_element_type=jnp.float32)
        * score_scale
    )
    valid = jnp.arange(count, dtype=jnp.int32) < length
    top = jnp.max(jnp.where(valid[None, :], scores, masked_score), axis=-1)
    weights = jnp.where(valid[None, :], jnp.exp(scores - top[:, None]), 0.0)
    totals, rounded = lax.optimization_barrier(
        (jnp.sum(weights, axis=-1), weights.astype(jnp.bfloat16))
    )
    context = jnp.einsum("qk,dk->dq", rounded, value_rows, preferred_element_type=jnp.float32)
    return (context / totals[None, :]).astype(jnp.bfloat16)


def sublayer(current, length, qkv_mine, qkv_other, out_full, gain, shift, out_shift, layer_scale,
             projected=None):
    tok_rows, width = current.shape
    head_width = width // HEADS
    ctx_count = lax.axis_size("ctx")
    core = lax.axis_index("ctx") % 2
    half = width // 2
    if projected is None:
        normed = normalize(current, gain, shift)
        normed_mine = lax.dynamic_slice_in_dim(normed, core * half, half, axis=1)
        normed_other = lax.dynamic_slice_in_dim(normed, (1 - core) * half, half, axis=1)
        projected = jnp.dot(normed_mine, qkv_mine, preferred_element_type=jnp.float32) + jnp.dot(
            normed_other, qkv_other, preferred_element_type=jnp.float32
        )
        projected = unrotate(projected.astype(jnp.bfloat16), "dp")
        projected = jnp.transpose(
            projected.reshape(tok_rows, 3, HEADS, head_width), (2, 1, 3, 0)
        )
    gathered = lax.all_to_all(projected, "ctx", 0, 3, tiled=True)
    context = head_attention(gathered[0], length, head_width ** (-0.5))
    context = jnp.transpose(context.reshape(head_width, ctx_count, tok_rows), (1, 0, 2))
    spread = lax.all_to_all(context, "ctx", 0, 0, tiled=True).reshape(width, tok_rows)
    mixed = jnp.einsum("ft,fo->to", spread, out_full, preferred_element_type=jnp.float32)
    mixed = mixed + out_shift
    return (current.astype(jnp.float32) + layer_scale * mixed).astype(jnp.bfloat16)


def ring_gather(piece, axis, on_block, made_axis=1):
    count = lax.axis_size(axis)
    right = [(i, (i + 1) % count) for i in range(count)]
    left = [(i, (i - 1) % count) for i in range(count)]
    blocks = [None] * count
    made = [None] * count
    blocks[0], made[0] = piece, on_block(piece)
    forward, backward = piece, piece
    for step in range(count // 2):
        forward = lax.ppermute(forward, axis, right)
        k = count - 1 - step
        blocks[k], made[k] = forward, on_block(forward)
        if step < (count - 1) // 2:
            backward = lax.ppermute(backward, axis, left)
            k = 1 + step
            blocks[k], made[k] = backward, on_block(backward)
    return jnp.concatenate(blocks, axis=1), jnp.concatenate(made, axis=made_axis)


def unrotate(rotated, axis, along=1):
    count = lax.axis_size(axis)
    cols = rotated.shape[along]
    shift = lax.axis_index(axis) * (cols // count)
    doubled = jnp.concatenate([rotated, rotated], axis=along)
    return lax.dynamic_slice_in_dim(doubled, cols - shift, cols, axis=along)


def per_device(patches, lengths, norm_gain, norm_bias, w_qkv, w_out, out_bias, scale_gain):
    section_index = lax.axis_index("pipe")
    section_count = lax.axis_size("pipe")
    core = lax.axis_index("ctx") % 2
    width = w_qkv.shape[1]
    half = width // 2
    rows_mine = lax.dynamic_slice_in_dim(w_qkv[0], core * half, half, axis=0)
    sibling = [(i, i ^ 1) for i in range(lax.axis_size("ctx"))]
    current = patches[0, 0]
    normed = normalize(current, norm_gain[0], norm_bias[0])
    normed_sibling = lax.ppermute(normed, "ctx", sibling)
    mine_rows = lax.dynamic_slice_in_dim(normed, core * half, half, axis=1)
    sibling_rows = lax.dynamic_slice_in_dim(normed_sibling, core * half, half, axis=1)

    both = jnp.stack([mine_rows, sibling_rows])

    def on_block(block):
        return jnp.einsum("kc,stk->sct", block, both, preferred_element_type=jnp.float32)

    qkv_mine, partial = ring_gather(rows_mine, "dp", on_block, made_axis=1)
    tok_rows = current.shape[0]
    partial_other = lax.ppermute(partial[1], "ctx", sibling)
    first = unrotate((partial[0] + partial_other).astype(jnp.bfloat16), "dp", along=0)
    first = jnp.transpose(first.reshape(3, HEADS, width // HEADS, tok_rows), (1, 0, 2, 3))
    qkv_other = lax.ppermute(qkv_mine, "ctx", sibling)
    args = (qkv_mine, qkv_other, w_out[0], norm_gain[0], norm_bias[0], out_bias[0], scale_gain[0])
    length = lengths[0, 0]
    outputs = []
    for turn_index in range(section_count):
        produced = sublayer(current, length, *args, projected=first if turn_index == 0 else None)
        outputs.append(produced)
        if turn_index + 1 < section_count:
            pairs = [(i, i + 1) for i in range(section_count - 1)]
            current = lax.ppermute(produced, "pipe", pairs)
    result = outputs[0]
    for turn_index in range(1, section_count):
        result = jnp.where(section_index == turn_index, outputs[turn_index], result)
    return result[None, None, None]


def solution(mesh):
    in_specs = (
        P(None, "dp", "ctx", None),
        P(None, "dp"),
        P("pipe", None),
        P("pipe", None),
        P("pipe", None, "dp"),
        P("pipe", None, None),
        P("pipe", None),
        P("pipe", None),
    )
    out_specs = P("pipe", None, "dp", "ctx", None)
    return jax.shard_map(
        per_device, mesh=mesh, in_specs=in_specs, out_specs=out_specs, check_vma=False
    )
```

```python
import jax
import jax.numpy as jnp
from jax import lax
from jax.sharding import PartitionSpec as P

HEADS = 16


epsilon = 1e-06
masked_score = -1e30


def normalize(hidden, gain, shift):
    values = hidden.astype(jnp.float32)
    row_mean = jnp.mean(values, axis=-1, keepdims=True)
    centered = values - row_mean
    variance = jnp.mean(centered * centered, axis=-1, keepdims=True)
    return (centered * lax.rsqrt(variance + epsilon) * gain + shift).astype(jnp.bfloat16)


def head_attention(qkv, length, score_scale):
    queries, key_rows, value_rows = qkv[0], qkv[1], qkv[2]
    count = qkv.shape[-1]
    scores = (
        jnp.einsum("dq,dk->qk", queries, key_rows, preferred_element_type=jnp.float32)
        * score_scale
    )
    valid = jnp.arange(count, dtype=jnp.int32) < length
    top = jnp.max(jnp.where(valid[None, :], scores, masked_score), axis=-1)
    weights = jnp.where(valid[None, :], jnp.exp(scores - top[:, None]), 0.0)
    totals, rounded = lax.optimization_barrier(
        (jnp.sum(weights, axis=-1), weights.astype(jnp.bfloat16))
    )
    context = jnp.einsum("qk,dk->dq", rounded, value_rows, preferred_element_type=jnp.float32)
    return (context / totals[None, :]).astype(jnp.bfloat16)


def sublayer(current, length, qkv_mine, qkv_other, out_full, gain, shift, out_shift, layer_scale,
             projected=None):
    tok_rows, width = current.shape
    head_width = width // HEADS
    ctx_count = lax.axis_size("ctx")
    core = lax.axis_index("ctx") % 2
    half = width // 2
    if projected is None:
        normed = normalize(current, gain, shift)
        normed_mine = lax.dynamic_slice_in_dim(normed, core * half, half, axis=1)
        normed_other = lax.dynamic_slice_in_dim(normed, (1 - core) * half, half, axis=1)
        projected = jnp.dot(normed_mine, qkv_mine, preferred_element_type=jnp.float32) + jnp.dot(
            normed_other, qkv_other, preferred_element_type=jnp.float32
        )
        projected = jnp.transpose(
            projected.astype(jnp.bfloat16).reshape(tok_rows, HEADS, 3, head_width), (1, 2, 3, 0)
        )
    gathered = lax.all_to_all(projected, "ctx", 0, 3, tiled=True)
    context = head_attention(gathered[0], length, head_width ** (-0.5))
    context = jnp.transpose(context.reshape(head_width, ctx_count, tok_rows), (1, 0, 2))
    spread = lax.all_to_all(context, "ctx", 0, 0, tiled=True).reshape(width, tok_rows)
    mixed = jnp.einsum("ft,fo->to", spread, out_full, preferred_element_type=jnp.float32)
    mixed = mixed + out_shift
    return (current.astype(jnp.float32) + layer_scale * mixed).astype(jnp.bfloat16)


def ring_gather(piece, axis, on_block, made_axis=1):
    count = lax.axis_size(axis)
    right = [(i, (i + 1) % count) for i in range(count)]
    left = [(i, (i - 1) % count) for i in range(count)]
    blocks = [None] * count
    made = [None] * count
    blocks[0], made[0] = piece, on_block(piece)
    forward, backward = piece, piece
    for step in range(count // 2):
        forward = lax.ppermute(forward, axis, right)
        k = count - 1 - step
        blocks[k], made[k] = forward, on_block(forward)
        if step < (count - 1) // 2:
            backward = lax.ppermute(backward, axis, left)
            k = 1 + step
            blocks[k], made[k] = backward, on_block(backward)
    return jnp.concatenate(blocks, axis=1), jnp.concatenate(made, axis=made_axis)


def unrotate(rotated, axis, along=1):
    count = lax.axis_size(axis)
    cols = rotated.shape[along]
    shift = lax.axis_index(axis) * (cols // count)
    doubled = jnp.concatenate([rotated, rotated], axis=along)
    return lax.dynamic_slice_in_dim(doubled, cols - shift, cols, axis=along)


def per_device(patches, lengths, norm_gain, norm_bias, w_qkv, w_out, out_bias, scale_gain):
    section_index = lax.axis_index("pipe")
    section_count = lax.axis_size("pipe")
    core = lax.axis_index("ctx") % 2
    width = w_qkv.shape[1]
    half = width // 2
    rows_mine = lax.dynamic_slice_in_dim(w_qkv[0], core * half, half, axis=0)
    sibling = [(i, i ^ 1) for i in range(lax.axis_size("ctx"))]
    current = patches[0, 0]
    normed = normalize(current, norm_gain[0], norm_bias[0])
    normed_sibling = lax.ppermute(normed, "ctx", sibling)
    mine_rows = lax.dynamic_slice_in_dim(normed, core * half, half, axis=1)
    sibling_rows = lax.dynamic_slice_in_dim(normed_sibling, core * half, half, axis=1)

    both = jnp.stack([mine_rows, sibling_rows])

    def on_block(block):
        return jnp.einsum("kc,stk->sct", block, both, preferred_element_type=jnp.float32)

    qkv_mine, partial = ring_gather(rows_mine, "dp", on_block, made_axis=1)
    tok_rows = current.shape[0]
    partial_other = lax.ppermute(partial[1], "ctx", sibling)
    first = unrotate((partial[0] + partial_other).astype(jnp.bfloat16), "dp", along=0)
    first = jnp.transpose(first.reshape(3, HEADS, width // HEADS, tok_rows), (1, 0, 2, 3))
    qkv_mine = unrotate(qkv_mine, "dp").reshape(half, 3, HEADS, width // HEADS)
    qkv_mine = jnp.transpose(qkv_mine, (0, 2, 1, 3)).reshape(half, 3 * width)
    qkv_other = lax.ppermute(qkv_mine, "ctx", sibling)
    args = (qkv_mine, qkv_other, w_out[0], norm_gain[0], norm_bias[0], out_bias[0], scale_gain[0])
    length = lengths[0, 0]
    outputs = []
    for turn_index in range(section_count):
        produced = sublayer(current, length, *args, projected=first if turn_index == 0 else None)
        outputs.append(produced)
        if turn_index + 1 < section_count:
            pairs = [(i, i + 1) for i in range(section_count - 1)]
            current = lax.ppermute(produced, "pipe", pairs)
    result = outputs[0]
    for turn_index in range(1, section_count):
        result = jnp.where(section_index == turn_index, outputs[turn_index], result)
    return result[None, None, None]


def solution(mesh):
    in_specs = (
        P(None, "dp", "ctx", None),
        P(None, "dp"),
        P("pipe", None),
        P("pipe", None),
        P("pipe", None, "dp"),
        P("pipe", None, None),
        P("pipe", None),
        P("pipe", None),
    )
    out_specs = P("pipe", None, "dp", "ctx", None)
    return jax.shard_map(
        per_device, mesh=mesh, in_specs=in_specs, out_specs=out_specs, check_vma=False
    )
```

```python
import jax
import jax.numpy as jnp
from jax import lax
from jax.sharding import PartitionSpec as P

HEADS = 16


epsilon = 1e-06
masked_score = -1e30


def normalize(hidden, gain, shift):
    values = hidden.astype(jnp.float32)
    row_mean = jnp.mean(values, axis=-1, keepdims=True)
    centered = values - row_mean
    variance = jnp.mean(centered * centered, axis=-1, keepdims=True)
    return (centered * lax.rsqrt(variance + epsilon) * gain + shift).astype(jnp.bfloat16)


def head_attention(qkv, length, score_scale):
    queries, key_rows, value_rows = qkv[0], qkv[1], qkv[2]
    count = qkv.shape[-1]
    scores = (
        jnp.einsum("dq,dk->qk", queries, key_rows, preferred_element_type=jnp.float32)
        * score_scale
    )
    valid = jnp.arange(count, dtype=jnp.int32) < length
    top = jnp.max(jnp.where(valid[None, :], scores, masked_score), axis=-1)
    weights = jnp.where(valid[None, :], jnp.exp(scores - top[:, None]), 0.0)
    totals, rounded = lax.optimization_barrier(
        (jnp.sum(weights, axis=-1), weights.astype(jnp.bfloat16))
    )
    context = jnp.einsum("qk,dk->dq", rounded, value_rows, preferred_element_type=jnp.float32)
    return (context / totals[None, :]).astype(jnp.bfloat16)


def sublayer(current, length, qkv_mine, qkv_other, out_full, gain, shift, out_shift, layer_scale,
             projected=None):
    tok_rows, width = current.shape
    head_width = width // HEADS
    ctx_count = lax.axis_size("ctx")
    core = lax.axis_index("ctx") % 2
    half = width // 2
    if projected is None:
        normed = normalize(current, gain, shift)
        normed_mine = lax.dynamic_slice_in_dim(normed, core * half, half, axis=1)
        normed_other = lax.dynamic_slice_in_dim(normed, (1 - core) * half, half, axis=1)
        projected = jnp.dot(normed_mine, qkv_mine, preferred_element_type=jnp.float32) + jnp.dot(
            normed_other, qkv_other, preferred_element_type=jnp.float32
        )
        projected = unrotate(projected.astype(jnp.bfloat16), "dp")
        projected = jnp.transpose(
            projected.reshape(tok_rows, 3, HEADS, head_width), (2, 1, 3, 0)
        )
    gathered = lax.all_to_all(projected, "ctx", 0, 3, tiled=True)
    context = head_attention(gathered[0], length, head_width ** (-0.5))
    context = jnp.transpose(context.reshape(head_width, ctx_count, tok_rows), (1, 0, 2))
    spread = lax.all_to_all(context, "ctx", 0, 0, tiled=True).reshape(width, tok_rows)
    mixed = jnp.einsum("ft,fo->to", spread, out_full, preferred_element_type=jnp.float32)
    mixed = mixed + out_shift
    return (current.astype(jnp.float32) + layer_scale * mixed).astype(jnp.bfloat16)


def ring_gather(piece, axis, on_block, made_axis=1):
    count = lax.axis_size(axis)
    right = [(i, (i + 1) % count) for i in range(count)]
    left = [(i, (i - 1) % count) for i in range(count)]
    blocks = [None] * count
    made = [None] * count
    blocks[0], made[0] = piece, on_block(piece)
    forward, backward = piece, piece
    for step in range(count // 2):
        forward = lax.ppermute(forward, axis, right)
        k = count - 1 - step
        blocks[k], made[k] = forward, on_block(forward)
        if step < (count - 1) // 2:
            backward = lax.ppermute(backward, axis, left)
            k = 1 + step
            blocks[k], made[k] = backward, on_block(backward)
    if made_axis is None:
        return jnp.concatenate(blocks, axis=1), made
    return jnp.concatenate(blocks, axis=1), jnp.concatenate(made, axis=made_axis)


def unrotate(rotated, axis, along=1):
    count = lax.axis_size(axis)
    cols = rotated.shape[along]
    shift = lax.axis_index(axis) * (cols // count)
    doubled = jnp.concatenate([rotated, rotated], axis=along)
    return lax.dynamic_slice_in_dim(doubled, cols - shift, cols, axis=along)


def per_device(patches, lengths, norm_gain, norm_bias, w_qkv, w_out, out_bias, scale_gain):
    section_index = lax.axis_index("pipe")
    section_count = lax.axis_size("pipe")
    core = lax.axis_index("ctx") % 2
    width = w_qkv.shape[1]
    half = width // 2
    rows_mine = lax.dynamic_slice_in_dim(w_qkv[0], core * half, half, axis=0)
    sibling = [(i, i ^ 1) for i in range(lax.axis_size("ctx"))]
    current = patches[0, 0]
    normed = normalize(current, norm_gain[0], norm_bias[0])
    normed_sibling = lax.ppermute(normed, "ctx", sibling)
    mine_rows = lax.dynamic_slice_in_dim(normed, core * half, half, axis=1)
    sibling_rows = lax.dynamic_slice_in_dim(normed_sibling, core * half, half, axis=1)

    tok_rows = current.shape[0]
    head_width = width // HEADS
    dp_count = lax.axis_size("dp")
    shard_segments = 3 * HEADS // dp_count

    def on_block(block):
        own = jnp.dot(mine_rows, block, preferred_element_type=jnp.float32)
        theirs = jnp.dot(sibling_rows, block, preferred_element_type=jnp.float32)
        summed = (own + lax.ppermute(theirs, "ctx", sibling)).astype(jnp.bfloat16)
        return (jnp.transpose(summed.reshape(tok_rows, shard_segments, head_width), (1, 2, 0)),)

    qkv_mine, made = ring_gather(rows_mine, "dp", on_block, made_axis=None)
    dp_index = lax.axis_index("dp")
    flat = jnp.zeros((3 * HEADS, head_width, tok_rows), jnp.bfloat16)
    for k, (segments,) in enumerate(made):
        owner = (dp_index + k) % dp_count
        flat = lax.dynamic_update_slice_in_dim(flat, segments, owner * shard_segments, axis=0)
    first = jnp.transpose(flat.reshape(3, HEADS, head_width, tok_rows), (1, 0, 2, 3))
    qkv_other = lax.ppermute(qkv_mine, "ctx", sibling)
    args = (qkv_mine, qkv_other, w_out[0], norm_gain[0], norm_bias[0], out_bias[0], scale_gain[0])
    length = lengths[0, 0]
    outputs = []
    for turn_index in range(section_count):
        produced = sublayer(current, length, *args, projected=first if turn_index == 0 else None)
        outputs.append(produced)
        if turn_index + 1 < section_count:
            pairs = [(i, i + 1) for i in range(section_count - 1)]
            current = lax.ppermute(produced, "pipe", pairs)
    result = outputs[0]
    for turn_index in range(1, section_count):
        result = jnp.where(section_index == turn_index, outputs[turn_index], result)
    return result[None, None, None]


def solution(mesh):
    in_specs = (
        P(None, "dp", "ctx", None),
        P(None, "dp"),
        P("pipe", None),
        P("pipe", None),
        P("pipe", None, "dp"),
        P("pipe", None, None),
        P("pipe", None),
        P("pipe", None),
    )
    out_specs = P("pipe", None, "dp", "ctx", None)
    return jax.shard_map(
        per_device, mesh=mesh, in_specs=in_specs, out_specs=out_specs, check_vma=False
    )
```

```python
import jax
import jax.numpy as jnp
from jax import lax
from jax.sharding import PartitionSpec as P

HEADS = 16


epsilon = 1e-06
masked_score = -1e30


def normalize(hidden, gain, shift):
    values = hidden.astype(jnp.float32)
    row_mean = jnp.mean(values, axis=-1, keepdims=True)
    centered = values - row_mean
    variance = jnp.mean(centered * centered, axis=-1, keepdims=True)
    return (centered * lax.rsqrt(variance + epsilon) * gain + shift).astype(jnp.bfloat16)


def head_attention(qkv, length, score_scale):
    queries, key_rows, value_rows = qkv[0], qkv[1], qkv[2]
    count = qkv.shape[-1]
    scores = (
        jnp.einsum("dq,dk->qk", queries, key_rows, preferred_element_type=jnp.float32)
        * score_scale
    )
    valid = jnp.arange(count, dtype=jnp.int32) < length
    top = jnp.max(jnp.where(valid[None, :], scores, masked_score), axis=-1)
    weights = jnp.where(valid[None, :], jnp.exp(scores - top[:, None]), 0.0)
    totals, rounded = lax.optimization_barrier(
        (jnp.sum(weights, axis=-1), weights.astype(jnp.bfloat16))
    )
    context = jnp.einsum("qk,dk->dq", rounded, value_rows, preferred_element_type=jnp.float32)
    return (context / totals[None, :]).astype(jnp.bfloat16)


def sublayer(current, length, qkv_mine, qkv_other, out_full, gain, shift, out_shift, layer_scale,
             projected=None):
    tok_rows, width = current.shape
    head_width = width // HEADS
    ctx_count = lax.axis_size("ctx")
    core = lax.axis_index("ctx") % 2
    half = width // 2
    if projected is None:
        normed = normalize(current, gain, shift)
        normed_mine = lax.dynamic_slice_in_dim(normed, core * half, half, axis=1)
        normed_other = lax.dynamic_slice_in_dim(normed, (1 - core) * half, half, axis=1)
        projected = jnp.dot(normed_mine, qkv_mine, preferred_element_type=jnp.float32) + jnp.dot(
            normed_other, qkv_other, preferred_element_type=jnp.float32
        )
        projected = unrotate(projected.astype(jnp.bfloat16), "dp")
        projected = jnp.transpose(
            projected.reshape(tok_rows, 3, HEADS, head_width), (2, 1, 3, 0)
        )
    gathered = lax.all_to_all(projected, "ctx", 0, 3, tiled=True)
    context = head_attention(gathered[0], length, head_width ** (-0.5))
    context = jnp.transpose(context.reshape(head_width, ctx_count, tok_rows), (1, 0, 2))
    spread = lax.all_to_all(context, "ctx", 0, 0, tiled=True).reshape(width, tok_rows)
    mixed = jnp.einsum("ft,fo->to", spread, out_full, preferred_element_type=jnp.float32)
    mixed = mixed + out_shift
    return (current.astype(jnp.float32) + layer_scale * mixed).astype(jnp.bfloat16)


def ring_gather(piece, axis, on_block, made_axis=1):
    count = lax.axis_size(axis)
    right = [(i, (i + 1) % count) for i in range(count)]
    left = [(i, (i - 1) % count) for i in range(count)]
    blocks = [None] * count
    made = [None] * count
    blocks[0], made[0] = piece, on_block(piece)
    forward, backward = piece, piece
    for step in range(count // 2):
        forward = lax.ppermute(forward, axis, right)
        k = count - 1 - step
        blocks[k], made[k] = forward, on_block(forward)
        if step < (count - 1) // 2:
            backward = lax.ppermute(backward, axis, left)
            k = 1 + step
            blocks[k], made[k] = backward, on_block(backward)
    blocks = lax.optimization_barrier(blocks)
    return jnp.concatenate(blocks, axis=1), jnp.concatenate(made, axis=made_axis)


def unrotate(rotated, axis, along=1):
    count = lax.axis_size(axis)
    cols = rotated.shape[along]
    shift = lax.axis_index(axis) * (cols // count)
    doubled = jnp.concatenate([rotated, rotated], axis=along)
    return lax.dynamic_slice_in_dim(doubled, cols - shift, cols, axis=along)


def per_device(patches, lengths, norm_gain, norm_bias, w_qkv, w_out, out_bias, scale_gain):
    section_index = lax.axis_index("pipe")
    section_count = lax.axis_size("pipe")
    core = lax.axis_index("ctx") % 2
    width = w_qkv.shape[1]
    half = width // 2
    rows_mine = lax.dynamic_slice_in_dim(w_qkv[0], core * half, half, axis=0)
    sibling = [(i, i ^ 1) for i in range(lax.axis_size("ctx"))]
    current = patches[0, 0]
    normed = normalize(current, norm_gain[0], norm_bias[0])
    normed_sibling = lax.ppermute(normed, "ctx", sibling)
    mine_rows = lax.dynamic_slice_in_dim(normed, core * half, half, axis=1)
    sibling_rows = lax.dynamic_slice_in_dim(normed_sibling, core * half, half, axis=1)

    both = jnp.stack([mine_rows, sibling_rows])

    def on_block(block):
        return jnp.einsum("kc,stk->sct", block, both, preferred_element_type=jnp.float32)

    qkv_mine, partial = ring_gather(rows_mine, "dp", on_block, made_axis=1)
    tok_rows = current.shape[0]
    partial_other = lax.ppermute(partial[1], "ctx", sibling)
    first = unrotate((partial[0] + partial_other).astype(jnp.bfloat16), "dp", along=0)
    first = jnp.transpose(first.reshape(3, HEADS, width // HEADS, tok_rows), (1, 0, 2, 3))
    qkv_other = lax.ppermute(qkv_mine, "ctx", sibling)
    args = (qkv_mine, qkv_other, w_out[0], norm_gain[0], norm_bias[0], out_bias[0], scale_gain[0])
    length = lengths[0, 0]
    outputs = []
    for turn_index in range(section_count):
        produced = sublayer(current, length, *args, projected=first if turn_index == 0 else None)
        outputs.append(produced)
        if turn_index + 1 < section_count:
            pairs = [(i, i + 1) for i in range(section_count - 1)]
            current = lax.ppermute(produced, "pipe", pairs)
    result = outputs[0]
    for turn_index in range(1, section_count):
        result = jnp.where(section_index == turn_index, outputs[turn_index], result)
    return result[None, None, None]


def solution(mesh):
    in_specs = (
        P(None, "dp", "ctx", None),
        P(None, "dp"),
        P("pipe", None),
        P("pipe", None),
        P("pipe", None, "dp"),
        P("pipe", None, None),
        P("pipe", None),
        P("pipe", None),
    )
    out_specs = P("pipe", None, "dp", "ctx", None)
    return jax.shard_map(
        per_device, mesh=mesh, in_specs=in_specs, out_specs=out_specs, check_vma=False
    )
```

```python
import jax
import jax.numpy as jnp
from jax import lax
from jax.sharding import PartitionSpec as P

HEADS = 16


epsilon = 1e-06
masked_score = -1e30


def normalize(hidden, gain, shift):
    values = hidden.astype(jnp.float32)
    row_mean = jnp.mean(values, axis=-1, keepdims=True)
    centered = values - row_mean
    variance = jnp.mean(centered * centered, axis=-1, keepdims=True)
    return (centered * lax.rsqrt(variance + epsilon) * gain + shift).astype(jnp.bfloat16)


def head_attention(qkv, length, score_scale):
    queries, key_rows, value_rows = qkv[0], qkv[1], qkv[2]
    count = qkv.shape[-1]
    scores = (
        jnp.einsum("dq,dk->qk", queries, key_rows, preferred_element_type=jnp.float32)
        * score_scale
    )
    valid = jnp.arange(count, dtype=jnp.int32) < length
    top = jnp.max(jnp.where(valid[None, :], scores, masked_score), axis=-1)
    weights = jnp.where(valid[None, :], jnp.exp(scores - top[:, None]), 0.0)
    totals, rounded = lax.optimization_barrier(
        (jnp.sum(weights, axis=-1), weights.astype(jnp.bfloat16))
    )
    context = jnp.einsum("qk,dk->dq", rounded, value_rows, preferred_element_type=jnp.float32)
    return (context / totals[None, :]).astype(jnp.bfloat16)


def sublayer(current, length, qkv_mine, qkv_other, out_full, gain, shift, out_shift, layer_scale,
             projected=None):
    tok_rows, width = current.shape
    head_width = width // HEADS
    ctx_count = lax.axis_size("ctx")
    core = lax.axis_index("ctx") % 2
    half = width // 2
    if projected is None:
        normed = normalize(current, gain, shift)
        normed_mine = lax.dynamic_slice_in_dim(normed, core * half, half, axis=1)
        normed_other = lax.dynamic_slice_in_dim(normed, (1 - core) * half, half, axis=1)
        projected = jnp.dot(normed_mine, qkv_mine, preferred_element_type=jnp.float32) + jnp.dot(
            normed_other, qkv_other, preferred_element_type=jnp.float32
        )
        projected = unrotate(projected.astype(jnp.bfloat16), "dp")
        projected = jnp.transpose(
            projected.reshape(tok_rows, 3, HEADS, head_width), (2, 1, 3, 0)
        )
    gathered = lax.all_to_all(projected, "ctx", 0, 3, tiled=True)
    context = head_attention(gathered[0], length, head_width ** (-0.5))
    context = jnp.transpose(context.reshape(head_width, ctx_count, tok_rows), (1, 0, 2))
    spread = lax.all_to_all(context, "ctx", 0, 0, tiled=True).reshape(width, tok_rows)
    mixed = jnp.einsum("ft,fo->to", spread, out_full, preferred_element_type=jnp.float32)
    mixed = mixed + out_shift
    return (current.astype(jnp.float32) + layer_scale * mixed).astype(jnp.bfloat16)


def ring_gather(piece, axis, on_block, made_axis=1):
    count = lax.axis_size(axis)
    right = [(i, (i + 1) % count) for i in range(count)]
    left = [(i, (i - 1) % count) for i in range(count)]
    blocks = [None] * count
    made = [None] * count
    blocks[0], made[0] = piece, on_block(piece)
    forward, backward = piece, piece
    for step in range(count // 2):
        forward = lax.ppermute(forward, axis, right)
        k = count - 1 - step
        blocks[k], made[k] = forward, on_block(forward)
        if step < (count - 1) // 2:
            backward = lax.ppermute(backward, axis, left)
            k = 1 + step
            blocks[k], made[k] = backward, on_block(backward)
    blocks = lax.optimization_barrier(blocks)
    if made_axis is None:
        return jnp.concatenate(blocks, axis=1), made
    return jnp.concatenate(blocks, axis=1), jnp.concatenate(made, axis=made_axis)


def unrotate(rotated, axis, along=1):
    count = lax.axis_size(axis)
    cols = rotated.shape[along]
    shift = lax.axis_index(axis) * (cols // count)
    doubled = jnp.concatenate([rotated, rotated], axis=along)
    return lax.dynamic_slice_in_dim(doubled, cols - shift, cols, axis=along)


def per_device(patches, lengths, norm_gain, norm_bias, w_qkv, w_out, out_bias, scale_gain):
    section_index = lax.axis_index("pipe")
    section_count = lax.axis_size("pipe")
    core = lax.axis_index("ctx") % 2
    width = w_qkv.shape[1]
    half = width // 2
    rows_mine = lax.dynamic_slice_in_dim(w_qkv[0], core * half, half, axis=0)
    sibling = [(i, i ^ 1) for i in range(lax.axis_size("ctx"))]
    current = patches[0, 0]
    normed = normalize(current, norm_gain[0], norm_bias[0])
    normed_sibling = lax.ppermute(normed, "ctx", sibling)
    mine_rows = lax.dynamic_slice_in_dim(normed, core * half, half, axis=1)
    sibling_rows = lax.dynamic_slice_in_dim(normed_sibling, core * half, half, axis=1)

    both = jnp.stack([mine_rows, sibling_rows])

    def on_block(block):
        return jnp.einsum("stk,kc->stc", both, block, preferred_element_type=jnp.float32)

    qkv_mine, made = ring_gather(rows_mine, "dp", on_block, made_axis=None)
    dp_count = lax.axis_size("dp")
    dp_index = lax.axis_index("dp")
    shard_width = made[0].shape[-1]
    partial = jnp.zeros(made[0].shape[:-1] + (shard_width * dp_count,), jnp.float32)
    for k, piece in enumerate(made):
        owner = (dp_index + k) % dp_count
        partial = lax.dynamic_update_slice_in_dim(partial, piece, owner * shard_width, axis=2)
    tok_rows = current.shape[0]
    partial_other = lax.ppermute(partial[1], "ctx", sibling)
    first = (partial[0] + partial_other).astype(jnp.bfloat16)
    first = jnp.transpose(first.reshape(tok_rows, 3, HEADS, width // HEADS), (2, 1, 3, 0))
    qkv_other = lax.ppermute(qkv_mine, "ctx", sibling)
    args = (qkv_mine, qkv_other, w_out[0], norm_gain[0], norm_bias[0], out_bias[0], scale_gain[0])
    length = lengths[0, 0]
    outputs = []
    for turn_index in range(section_count):
        produced = sublayer(current, length, *args, projected=first if turn_index == 0 else None)
        outputs.append(produced)
        if turn_index + 1 < section_count:
            pairs = [(i, i + 1) for i in range(section_count - 1)]
            current = lax.ppermute(produced, "pipe", pairs)
    result = outputs[0]
    for turn_index in range(1, section_count):
        result = jnp.where(section_index == turn_index, outputs[turn_index], result)
    return result[None, None, None]


def solution(mesh):
    in_specs = (
        P(None, "dp", "ctx", None),
        P(None, "dp"),
        P("pipe", None),
        P("pipe", None),
        P("pipe", None, "dp"),
        P("pipe", None, None),
        P("pipe", None),
        P("pipe", None),
    )
    out_specs = P("pipe", None, "dp", "ctx", None)
    return jax.shard_map(
        per_device, mesh=mesh, in_specs=in_specs, out_specs=out_specs, check_vma=False
    )
```

```python
import jax
import jax.numpy as jnp
from jax import lax
from jax.sharding import PartitionSpec as P

HEADS = 16


epsilon = 1e-06
masked_score = -1e30


def normalize(hidden, gain, shift):
    values = hidden.astype(jnp.float32)
    row_mean = jnp.mean(values, axis=-1, keepdims=True)
    centered = values - row_mean
    variance = jnp.mean(centered * centered, axis=-1, keepdims=True)
    return (centered * lax.rsqrt(variance + epsilon) * gain + shift).astype(jnp.bfloat16)


def head_attention(qkv, length, score_scale):
    queries, key_rows, value_rows = qkv[0], qkv[1], qkv[2]
    count = qkv.shape[-1]
    scores = (
        jnp.einsum("dq,dk->qk", queries, key_rows, preferred_element_type=jnp.float32)
        * score_scale
    )
    valid = jnp.arange(count, dtype=jnp.int32) < length
    top = jnp.max(jnp.where(valid[None, :], scores, masked_score), axis=-1)
    weights = jnp.where(valid[None, :], jnp.exp(scores - top[:, None]), 0.0)
    totals, rounded = lax.optimization_barrier(
        (jnp.sum(weights, axis=-1), weights.astype(jnp.bfloat16))
    )
    context = jnp.einsum("qk,dk->dq", rounded, value_rows, preferred_element_type=jnp.float32)
    return (context / totals[None, :]).astype(jnp.bfloat16)


def sublayer(current, length, qkv_mine, qkv_other, out_full, gain, shift, out_shift, layer_scale,
             projected=None):
    tok_rows, width = current.shape
    head_width = width // HEADS
    ctx_count = lax.axis_size("ctx")
    core = lax.axis_index("ctx") % 2
    half = width // 2
    if projected is None:
        normed = normalize(current, gain, shift)
        normed_mine = lax.dynamic_slice_in_dim(normed, core * half, half, axis=1)
        normed_other = lax.dynamic_slice_in_dim(normed, (1 - core) * half, half, axis=1)
        projected = jnp.dot(normed_mine, qkv_mine, preferred_element_type=jnp.float32) + jnp.dot(
            normed_other, qkv_other, preferred_element_type=jnp.float32
        )
        projected = projected.astype(jnp.bfloat16)
        projected = jnp.transpose(
            projected.reshape(tok_rows, 3, HEADS, head_width), (2, 1, 3, 0)
        )
    gathered = lax.all_to_all(projected, "ctx", 0, 3, tiled=True)
    context = head_attention(gathered[0], length, head_width ** (-0.5))
    context = jnp.transpose(context.reshape(head_width, ctx_count, tok_rows), (1, 0, 2))
    spread = lax.all_to_all(context, "ctx", 0, 0, tiled=True).reshape(width, tok_rows)
    mixed = jnp.einsum("ft,fo->to", spread, out_full, preferred_element_type=jnp.float32)
    mixed = mixed + out_shift
    return (current.astype(jnp.float32) + layer_scale * mixed).astype(jnp.bfloat16)


def ring_gather(piece, axis, on_block):
    count = lax.axis_size(axis)
    right = [(i, (i + 1) % count) for i in range(count)]
    left = [(i, (i - 1) % count) for i in range(count)]
    blocks = [None] * count
    made = [None] * count
    blocks[0], made[0] = piece, on_block(piece)
    forward, backward = piece, piece
    for step in range(count // 2):
        forward = lax.ppermute(forward, axis, right)
        k = count - 1 - step
        blocks[k], made[k] = forward, on_block(forward)
        if step < (count - 1) // 2:
            backward = lax.ppermute(backward, axis, left)
            k = 1 + step
            blocks[k], made[k] = backward, on_block(backward)
    blocks = lax.optimization_barrier(blocks)
    index = lax.axis_index(axis)
    rows, cols = piece.shape
    whole = jnp.zeros((rows, cols * count), piece.dtype)
    for k, block in enumerate(blocks):
        whole = lax.dynamic_update_slice_in_dim(whole, block, ((index + k) % count) * cols, axis=1)
    return whole, made


def per_device(patches, lengths, norm_gain, norm_bias, w_qkv, w_out, out_bias, scale_gain):
    section_index = lax.axis_index("pipe")
    section_count = lax.axis_size("pipe")
    core = lax.axis_index("ctx") % 2
    width = w_qkv.shape[1]
    half = width // 2
    rows_mine = lax.dynamic_slice_in_dim(w_qkv[0], core * half, half, axis=0)
    sibling = [(i, i ^ 1) for i in range(lax.axis_size("ctx"))]
    current = patches[0, 0]
    normed = normalize(current, norm_gain[0], norm_bias[0])
    normed_sibling = lax.ppermute(normed, "ctx", sibling)
    mine_rows = lax.dynamic_slice_in_dim(normed, core * half, half, axis=1)
    sibling_rows = lax.dynamic_slice_in_dim(normed_sibling, core * half, half, axis=1)

    both = jnp.stack([mine_rows, sibling_rows])

    def on_block(block):
        return jnp.einsum("stk,kc->stc", both, block, preferred_element_type=jnp.float32)

    qkv_mine, made = ring_gather(rows_mine, "dp", on_block)
    dp_count = lax.axis_size("dp")
    dp_index = lax.axis_index("dp")
    shard_width = made[0].shape[-1]
    partial = jnp.zeros(made[0].shape[:-1] + (shard_width * dp_count,), jnp.float32)
    for k, piece in enumerate(made):
        owner = (dp_index + k) % dp_count
        partial = lax.dynamic_update_slice_in_dim(partial, piece, owner * shard_width, axis=2)
    tok_rows = current.shape[0]
    partial_other = lax.ppermute(partial[1], "ctx", sibling)
    first = (partial[0] + partial_other).astype(jnp.bfloat16)
    first = jnp.transpose(first.reshape(tok_rows, 3, HEADS, width // HEADS), (2, 1, 3, 0))
    qkv_other = lax.ppermute(qkv_mine, "ctx", sibling)
    args = (qkv_mine, qkv_other, w_out[0], norm_gain[0], norm_bias[0], out_bias[0], scale_gain[0])
    length = lengths[0, 0]
    outputs = []
    for turn_index in range(section_count):
        produced = sublayer(current, length, *args, projected=first if turn_index == 0 else None)
        outputs.append(produced)
        if turn_index + 1 < section_count:
            pairs = [(i, i + 1) for i in range(section_count - 1)]
            current = lax.ppermute(produced, "pipe", pairs)
    result = outputs[0]
    for turn_index in range(1, section_count):
        result = jnp.where(section_index == turn_index, outputs[turn_index], result)
    return result[None, None, None]


def solution(mesh):
    in_specs = (
        P(None, "dp", "ctx", None),
        P(None, "dp"),
        P("pipe", None),
        P("pipe", None),
        P("pipe", None, "dp"),
        P("pipe", None, None),
        P("pipe", None),
        P("pipe", None),
    )
    out_specs = P("pipe", None, "dp", "ctx", None)
    return jax.shard_map(
        per_device, mesh=mesh, in_specs=in_specs, out_specs=out_specs, check_vma=False
    )
```

```python
import jax
import jax.numpy as jnp
from jax import lax
from jax.sharding import PartitionSpec as P

HEADS = 16


epsilon = 1e-06
masked_score = -1e30


def normalize(hidden, gain, shift):
    values = hidden.astype(jnp.float32)
    row_mean = jnp.mean(values, axis=-1, keepdims=True)
    centered = values - row_mean
    variance = jnp.mean(centered * centered, axis=-1, keepdims=True)
    return (centered * lax.rsqrt(variance + epsilon) * gain + shift).astype(jnp.bfloat16)


def head_attention(qkv, length, score_scale):
    queries, key_rows, value_rows = qkv[0], qkv[1], qkv[2]
    count = qkv.shape[-1]
    scores = (
        jnp.einsum("dq,dk->qk", queries, key_rows, preferred_element_type=jnp.float32)
        * score_scale
    )
    valid = jnp.arange(count, dtype=jnp.int32) < length
    top = jnp.max(jnp.where(valid[None, :], scores, masked_score), axis=-1)
    weights = jnp.where(valid[None, :], jnp.exp(scores - top[:, None]), 0.0)
    totals, rounded = lax.optimization_barrier(
        (jnp.sum(weights, axis=-1), weights.astype(jnp.bfloat16))
    )
    context = jnp.einsum("qk,dk->dq", rounded, value_rows, preferred_element_type=jnp.float32)
    return (context / totals[None, :]).astype(jnp.bfloat16)


def sublayer(current, length, qkv_mine, qkv_other, out_full, gain, shift, out_shift, layer_scale,
             projected=None):
    tok_rows, width = current.shape
    head_width = width // HEADS
    ctx_count = lax.axis_size("ctx")
    core = lax.axis_index("ctx") % 2
    half = width // 2
    if projected is None:
        normed = normalize(current, gain, shift)
        normed_mine = lax.dynamic_slice_in_dim(normed, core * half, half, axis=1)
        normed_other = lax.dynamic_slice_in_dim(normed, (1 - core) * half, half, axis=1)
        projected = jnp.dot(normed_mine, qkv_mine, preferred_element_type=jnp.float32) + jnp.dot(
            normed_other, qkv_other, preferred_element_type=jnp.float32
        )
        segments = jnp.transpose(projected.astype(jnp.bfloat16)).reshape(-1, head_width, tok_rows)
        count = segments.shape[0]
        shift = lax.axis_index("dp") * (count // lax.axis_size("dp"))
        wanted = jnp.arange(HEADS)[:, None] + HEADS * jnp.arange(3)[None, :]
        projected = jnp.take(segments, ((wanted - shift) % count).reshape(-1), axis=0, mode="clip")
        projected = projected.reshape(HEADS, 3, head_width, tok_rows)
    gathered = lax.all_to_all(projected, "ctx", 0, 3, tiled=True)
    context = head_attention(gathered[0], length, head_width ** (-0.5))
    context = jnp.transpose(context.reshape(head_width, ctx_count, tok_rows), (1, 0, 2))
    spread = lax.all_to_all(context, "ctx", 0, 0, tiled=True).reshape(width, tok_rows)
    mixed = jnp.einsum("ft,fo->to", spread, out_full, preferred_element_type=jnp.float32)
    mixed = mixed + out_shift
    return (current.astype(jnp.float32) + layer_scale * mixed).astype(jnp.bfloat16)


def ring_gather(piece, axis, on_block, made_axis=1):
    count = lax.axis_size(axis)
    right = [(i, (i + 1) % count) for i in range(count)]
    left = [(i, (i - 1) % count) for i in range(count)]
    blocks = [None] * count
    made = [None] * count
    blocks[0], made[0] = piece, on_block(piece)
    forward, backward = piece, piece
    for step in range(count // 2):
        forward = lax.ppermute(forward, axis, right)
        k = count - 1 - step
        blocks[k], made[k] = forward, on_block(forward)
        if step < (count - 1) // 2:
            backward = lax.ppermute(backward, axis, left)
            k = 1 + step
            blocks[k], made[k] = backward, on_block(backward)
    blocks = lax.optimization_barrier(blocks)
    if made_axis is None:
        return jnp.concatenate(blocks, axis=1), made
    return jnp.concatenate(blocks, axis=1), jnp.concatenate(made, axis=made_axis)


def unrotate(rotated, axis, along=1):
    count = lax.axis_size(axis)
    cols = rotated.shape[along]
    shift = lax.axis_index(axis) * (cols // count)
    doubled = jnp.concatenate([rotated, rotated], axis=along)
    return lax.dynamic_slice_in_dim(doubled, cols - shift, cols, axis=along)


def per_device(patches, lengths, norm_gain, norm_bias, w_qkv, w_out, out_bias, scale_gain):
    section_index = lax.axis_index("pipe")
    section_count = lax.axis_size("pipe")
    core = lax.axis_index("ctx") % 2
    width = w_qkv.shape[1]
    half = width // 2
    rows_mine = lax.dynamic_slice_in_dim(w_qkv[0], core * half, half, axis=0)
    sibling = [(i, i ^ 1) for i in range(lax.axis_size("ctx"))]
    current = patches[0, 0]
    normed = normalize(current, norm_gain[0], norm_bias[0])
    normed_sibling = lax.ppermute(normed, "ctx", sibling)
    mine_rows = lax.dynamic_slice_in_dim(normed, core * half, half, axis=1)
    sibling_rows = lax.dynamic_slice_in_dim(normed_sibling, core * half, half, axis=1)

    both = jnp.stack([mine_rows, sibling_rows])

    def on_block(block):
        return jnp.einsum("stk,kc->stc", both, block, preferred_element_type=jnp.float32)

    qkv_mine, made = ring_gather(rows_mine, "dp", on_block, made_axis=None)
    dp_count = lax.axis_size("dp")
    dp_index = lax.axis_index("dp")
    shard_width = made[0].shape[-1]
    partial = jnp.zeros(made[0].shape[:-1] + (shard_width * dp_count,), jnp.float32)
    for k, piece in enumerate(made):
        owner = (dp_index + k) % dp_count
        partial = lax.dynamic_update_slice_in_dim(partial, piece, owner * shard_width, axis=2)
    tok_rows = current.shape[0]
    partial_other = lax.ppermute(partial[1], "ctx", sibling)
    first = (partial[0] + partial_other).astype(jnp.bfloat16)
    first = jnp.transpose(first.reshape(tok_rows, 3, HEADS, width // HEADS), (2, 1, 3, 0))
    qkv_other = lax.ppermute(qkv_mine, "ctx", sibling)
    args = (qkv_mine, qkv_other, w_out[0], norm_gain[0], norm_bias[0], out_bias[0], scale_gain[0])
    length = lengths[0, 0]
    outputs = []
    for turn_index in range(section_count):
        produced = sublayer(current, length, *args, projected=first if turn_index == 0 else None)
        outputs.append(produced)
        if turn_index + 1 < section_count:
            pairs = [(i, i + 1) for i in range(section_count - 1)]
            current = lax.ppermute(produced, "pipe", pairs)
    result = outputs[0]
    for turn_index in range(1, section_count):
        result = jnp.where(section_index == turn_index, outputs[turn_index], result)
    return result[None, None, None]


def solution(mesh):
    in_specs = (
        P(None, "dp", "ctx", None),
        P(None, "dp"),
        P("pipe", None),
        P("pipe", None),
        P("pipe", None, "dp"),
        P("pipe", None, None),
        P("pipe", None),
        P("pipe", None),
    )
    out_specs = P("pipe", None, "dp", "ctx", None)
    return jax.shard_map(
        per_device, mesh=mesh, in_specs=in_specs, out_specs=out_specs, check_vma=False
    )
```

```python
import jax
import jax.numpy as jnp
from jax import lax
from jax.sharding import PartitionSpec as P

HEADS = 16


epsilon = 1e-06
masked_score = -1e30


def normalize(hidden, gain, shift):
    values = hidden.astype(jnp.float32)
    row_mean = jnp.mean(values, axis=-1, keepdims=True)
    centered = values - row_mean
    variance = jnp.mean(centered * centered, axis=-1, keepdims=True)
    return (centered * lax.rsqrt(variance + epsilon) * gain + shift).astype(jnp.bfloat16)


def head_attention(qkv, length, score_scale):
    queries, key_rows, value_rows = qkv[0], qkv[1], qkv[2]
    count = qkv.shape[-1]
    scores = (
        jnp.einsum("dq,dk->qk", queries, key_rows, preferred_element_type=jnp.float32)
        * score_scale
    )
    valid = jnp.arange(count, dtype=jnp.int32) < length
    top = jnp.max(jnp.where(valid[None, :], scores, masked_score), axis=-1)
    weights = jnp.where(valid[None, :], jnp.exp(scores - top[:, None]), 0.0)
    totals, rounded = lax.optimization_barrier(
        (jnp.sum(weights, axis=-1), weights.astype(jnp.bfloat16))
    )
    context = jnp.einsum("qk,dk->dq", rounded, value_rows, preferred_element_type=jnp.float32)
    return (context / totals[None, :]).astype(jnp.bfloat16)


def sublayer(current, length, qkv_mine, qkv_other, out_full, gain, shift, out_shift, layer_scale,
             projected=None):
    tok_rows, width = current.shape
    head_width = width // HEADS
    ctx_count = lax.axis_size("ctx")
    core = lax.axis_index("ctx") % 2
    half = width // 2
    if projected is None:
        normed = normalize(current, gain, shift)
        normed_mine = lax.dynamic_slice_in_dim(normed, core * half, half, axis=1)
        normed_other = lax.dynamic_slice_in_dim(normed, (1 - core) * half, half, axis=1)
        projected = jnp.dot(normed_mine, qkv_mine, preferred_element_type=jnp.float32) + jnp.dot(
            normed_other, qkv_other, preferred_element_type=jnp.float32
        )
        projected = unrotate(jnp.transpose(projected.astype(jnp.bfloat16)), "dp", along=0)
        projected = jnp.transpose(
            projected.reshape(3, HEADS, head_width, tok_rows), (1, 0, 2, 3)
        )
    gathered = lax.all_to_all(projected, "ctx", 0, 3, tiled=True)
    context = head_attention(gathered[0], length, head_width ** (-0.5))
    context = jnp.transpose(context.reshape(head_width, ctx_count, tok_rows), (1, 0, 2))
    spread = lax.all_to_all(context, "ctx", 0, 0, tiled=True).reshape(width, tok_rows)
    mixed = jnp.einsum("ft,fo->to", spread, out_full, preferred_element_type=jnp.float32)
    mixed = mixed + out_shift
    return (current.astype(jnp.float32) + layer_scale * mixed).astype(jnp.bfloat16)


def ring_gather(piece, axis, on_block, made_axis=1):
    count = lax.axis_size(axis)
    right = [(i, (i + 1) % count) for i in range(count)]
    left = [(i, (i - 1) % count) for i in range(count)]
    blocks = [None] * count
    made = [None] * count
    blocks[0], made[0] = piece, on_block(piece)
    forward, backward = piece, piece
    for step in range(count // 2):
        forward = lax.ppermute(forward, axis, right)
        k = count - 1 - step
        blocks[k], made[k] = forward, on_block(forward)
        if step < (count - 1) // 2:
            backward = lax.ppermute(backward, axis, left)
            k = 1 + step
            blocks[k], made[k] = backward, on_block(backward)
    blocks = lax.optimization_barrier(blocks)
    if made_axis is None:
        return jnp.concatenate(blocks, axis=1), made
    return jnp.concatenate(blocks, axis=1), jnp.concatenate(made, axis=made_axis)


def unrotate(rotated, axis, along=1):
    count = lax.axis_size(axis)
    cols = rotated.shape[along]
    shift = lax.axis_index(axis) * (cols // count)
    doubled = jnp.concatenate([rotated, rotated], axis=along)
    return lax.dynamic_slice_in_dim(doubled, cols - shift, cols, axis=along)


def per_device(patches, lengths, norm_gain, norm_bias, w_qkv, w_out, out_bias, scale_gain):
    section_index = lax.axis_index("pipe")
    section_count = lax.axis_size("pipe")
    core = lax.axis_index("ctx") % 2
    width = w_qkv.shape[1]
    half = width // 2
    rows_mine = lax.dynamic_slice_in_dim(w_qkv[0], core * half, half, axis=0)
    sibling = [(i, i ^ 1) for i in range(lax.axis_size("ctx"))]
    current = patches[0, 0]
    normed = normalize(current, norm_gain[0], norm_bias[0])
    normed_sibling = lax.ppermute(normed, "ctx", sibling)
    mine_rows = lax.dynamic_slice_in_dim(normed, core * half, half, axis=1)
    sibling_rows = lax.dynamic_slice_in_dim(normed_sibling, core * half, half, axis=1)

    both = jnp.stack([mine_rows, sibling_rows])

    def on_block(block):
        return jnp.einsum("stk,kc->stc", both, block, preferred_element_type=jnp.float32)

    qkv_mine, made = ring_gather(rows_mine, "dp", on_block, made_axis=None)
    dp_count = lax.axis_size("dp")
    dp_index = lax.axis_index("dp")
    shard_width = made[0].shape[-1]
    partial = jnp.zeros(made[0].shape[:-1] + (shard_width * dp_count,), jnp.float32)
    for k, piece in enumerate(made):
        owner = (dp_index + k) % dp_count
        partial = lax.dynamic_update_slice_in_dim(partial, piece, owner * shard_width, axis=2)
    tok_rows = current.shape[0]
    partial_other = lax.ppermute(partial[1], "ctx", sibling)
    first = (partial[0] + partial_other).astype(jnp.bfloat16)
    first = jnp.transpose(first.reshape(tok_rows, 3, HEADS, width // HEADS), (2, 1, 3, 0))
    qkv_other = lax.ppermute(qkv_mine, "ctx", sibling)
    args = (qkv_mine, qkv_other, w_out[0], norm_gain[0], norm_bias[0], out_bias[0], scale_gain[0])
    length = lengths[0, 0]
    outputs = []
    for turn_index in range(section_count):
        produced = sublayer(current, length, *args, projected=first if turn_index == 0 else None)
        outputs.append(produced)
        if turn_index + 1 < section_count:
            pairs = [(i, i + 1) for i in range(section_count - 1)]
            current = lax.ppermute(produced, "pipe", pairs)
    result = outputs[0]
    for turn_index in range(1, section_count):
        result = jnp.where(section_index == turn_index, outputs[turn_index], result)
    return result[None, None, None]


def solution(mesh):
    in_specs = (
        P(None, "dp", "ctx", None),
        P(None, "dp"),
        P("pipe", None),
        P("pipe", None),
        P("pipe", None, "dp"),
        P("pipe", None, None),
        P("pipe", None),
        P("pipe", None),
    )
    out_specs = P("pipe", None, "dp", "ctx", None)
    return jax.shard_map(
        per_device, mesh=mesh, in_specs=in_specs, out_specs=out_specs, check_vma=False
    )
```
